128 devices in a mesh: head: 2 (over core), req: 64 (over x, y, z).
Axes of the slice: x: 4, y: 4, z: 4, core: 2. Of those that a mesh axis runs over, the one named last changes fastest.
Arguments:
- queries: bfloat16 [512, 8192], P('req', 'head'), may hold values from -9 to 9
- new_key: bfloat16 [512, 1024], P('req', 'head'), may hold values from -4 to 4
- new_value: bfloat16 [512, 1024], P('req', 'head'), may hold values from -4 to 4
- key_cache: bfloat16 [5888, 64, 1024], P('req', None, 'head'), may hold values from -4 to 4
- value_cache: bfloat16 [5888, 64, 1024], P('req', None, 'head'), may hold values from -4 to 4
- lengths: int32 [512], P('req'), may hold values from 1 to 4096, as said below
- page_table: int32 [512, 64], P('req'), may hold values from 0 to 91, as said below
- residual: bfloat16 [512, 8192], P(None, ('head', 'req')), may hold values from -6 to 6
- out_weight: bfloat16 [8192, 8192], P(None, ('head', 'req')), may hold values from -0.25 to 0.25
- gate_weight: bfloat16 [8192, 28672], P('head', 'req'), may hold values from -0.0625 to 0.0625
- up_weight: bfloat16 [8192, 28672], P('head', 'req'), may hold values from -0.0625 to 0.0625
- down_weight: bfloat16 [28672, 8192], P('req', 'head'), may hold values from -0.09375 to 0.09375
Outputs:
- layer_out: bfloat16 [512, 8192], P(None, ('head', 'req'))
The draws below stay inside these ranges and needn't reach their ends.
Inputs may be any that keep to these rules, and one draw needn't show every extreme that they name: `lengths`: the 8 requests of one index of req hold at most one request of length 4096 and all others at most 256; each such group holds one request of length exactly 256, and some group holds one of length 4096. `page_table`: for request r the first ceil(lengths[r] / 64) entries name distinct pages of the pool of index r // 8 of req, and no page serves two requests; the other entries are arbitrary offsets and are not read.
All inputs are finite; a program needn't handle non-finite values.
Results may differ from the reference program's by a relative error of at most 0.01.
Values may be sent and summed in bfloat16 or wider, within the bound.
No kernel may reach another device: no remote copies, remote signals or barrier semaphores. Data moves between devices by JAX's collectives and lax.ppermute only.
A program may use at most 192 MiB of HBM per device.

```python
import jax
import jax.numpy as jnp
from jax import lax

D = 8192
FF = 28672
QH = 64
KVH = 8
HD = 128
REQ_DEV = 8
PAGE = 64
LONG = 4096
SHORT = 256
PAGES_MAX = 64
POOL = 92
REQS = 512
N_REQ = 64


def draw_queries(key, part):
    sub_key = jax.random.fold_in(key, 21)
    base_draw = jnp.clip(jax.random.normal(sub_key, (REQS, QH * HD), jnp.float32), -4.0, 4.0)
    return base_draw.astype(jnp.bfloat16)


def draw_key_cache(key, part):
    rows_all = REQS // REQ_DEV * POOL
    sub_key = jax.random.fold_in(key, 41)
    base_draw = jnp.clip(jax.random.normal(sub_key, (rows_all, PAGE, KVH * HD), jnp.float32), -4.0, 4.0)
    return base_draw.astype(jnp.bfloat16)


def pool_order(sub_key):
    return jax.random.permutation(sub_key, POOL)


def pick_pages(permute, page_index):
    return permute[page_index]


def cache_layout(key):
    sub_keys = jax.random.split(jax.random.fold_in(key, 31), 6)
    devices = REQS // REQ_DEV
    chosen = jax.random.randint(sub_keys[0], (), 0, devices)
    has_long = (jax.random.randint(sub_keys[1], (devices,), 0, 5) < 2) | (jnp.arange(devices) == chosen)
    long_slot = jax.random.randint(sub_keys[2], (devices, 1), 0, REQ_DEV)
    short_slot = (long_slot + 1) % REQ_DEV
    slot_ids = jnp.arange(REQ_DEV).reshape(1, REQ_DEV)
    lengths = jax.random.randint(sub_keys[3], (devices, REQ_DEV), 1, SHORT + 1)
    lengths = jnp.where(slot_ids == short_slot, SHORT, lengths)
    lengths = jnp.where((slot_ids == long_slot) & has_long[:, None], LONG, lengths)
    used_pages = (lengths + PAGE - 1) // PAGE
    offsets = jnp.cumsum(used_pages, axis=1) - used_pages
    permutes = jax.vmap(pool_order)(jax.random.split(sub_keys[4], devices))
    slot_range = jnp.arange(PAGES_MAX).reshape(1, 1, PAGES_MAX)
    page_index = jnp.minimum(offsets[:, :, None] + slot_range, POOL - 1)
    live_pages = jax.vmap(pick_pages)(permutes, page_index)
    filler = jax.random.randint(sub_keys[5], (devices, REQ_DEV, PAGES_MAX), 0, POOL)
    table_out = jnp.where(slot_range < used_pages[:, :, None], live_pages, filler)
    return (lengths.reshape(REQS).astype(jnp.int32), table_out.reshape(REQS, PAGES_MAX).astype(jnp.int32))


def draw_lengths(key, part):
    return cache_layout(key)[0]


def draw_page_table(key, part):
    return cache_layout(key)[1]


def raised(drawn, own_key, source, target, blocks, factor):
    def block_of(axis_at):
        return (jnp.arange(drawn.shape[axis_at]) // (drawn.shape[axis_at] // blocks)).reshape((-1,) + (1,) * (drawn.ndim - 1 - axis_at))

    first = jax.random.permutation(own_key, blocks)[block_of(target)]
    other_side = (block_of(target) + blocks // 2) % blocks
    return jnp.where((block_of(source) == first) | (block_of(source) == other_side), factor * drawn, drawn)


def block_scale(key, dims, cuts, low, largest):
    loudness, own = 1.0, jax.random.fold_in(key, 6)
    for position, shards_of in cuts:
        steps = jnp.exp(jax.random.uniform(jax.random.fold_in(own, position), (shards_of,), jnp.float32, low / len(cuts), largest / len(cuts)))
        loudness = loudness * jnp.repeat(steps, dims[position] // shards_of).reshape([-1 if axis == position else 1 for axis in range(len(dims))])
    return loudness


def centred(key, extent, deviation, reach, cuts=(), held_as=jnp.bfloat16):
    result = deviation * jax.random.normal(key, extent, jnp.float32)
    if cuts:
        result = result * block_scale(key, extent, cuts, -0.22, 0.18)
    return jnp.clip(result, -reach, reach).astype(held_as)


def gaussian_with(stream_key, dims, deviation, limit, cuts, heavy, kind=jnp.bfloat16):
    drawn = deviation * jax.random.normal(stream_key, dims, jnp.float32)
    if cuts:
        drawn = drawn * block_scale(stream_key, dims, cuts, -0.22, 0.18)
    return jnp.clip(raised(drawn, jax.random.fold_in(stream_key, 3), *heavy), -limit, limit).astype(kind)


def setup_inputs(seed: int = 0) -> dict:
    arg_keys = jax.random.split(jax.random.key(seed), 13)
    return {
        "queries": draw_queries(jax.random.fold_in(arg_keys[12], 71), 0),
        "new_key": centred(arg_keys[1], (REQS, KVH * HD), 1.0, 4.0, ((0, 64), (1, 2))),
        "new_value": centred(arg_keys[2], (REQS, KVH * HD), 1.0, 4.0, ((0, 64), (1, 2))),
        "key_cache": draw_key_cache(jax.random.fold_in(arg_keys[12], 71), 0),
        "value_cache": centred(arg_keys[4], (N_REQ * POOL, PAGE, KVH * HD), 1.0, 4.0, ((0, 64), (2, 2))),
        "lengths": draw_lengths(jax.random.fold_in(arg_keys[12], 71), 0),
        "page_table": draw_page_table(jax.random.fold_in(arg_keys[12], 71), 0),
        "residual": centred(arg_keys[7], (REQS, D), 1.0, 6.0, ((1, 128),)),
        "out_weight": centred(arg_keys[8], (QH * HD, D), (4 * HD) ** -0.5, 0.25, ((1, 128),)),
        "gate_weight": centred(arg_keys[9], (D, FF), D ** -0.5, 0.0625, ((0, 2), (1, 64))),
        "up_weight": centred(arg_keys[10], (D, FF), D ** -0.5, 0.0625, ((0, 2), (1, 64))),
        "down_weight": gaussian_with(arg_keys[11], (FF, D), FF ** -0.5, 0.09375, ((0, 64), (1, 2)), (0, 1, 64, 4.0)),
    }


def attend_each(request_item, key_cache, value_cache):
    query_row, key_new, value_new, length, pages = request_item
    key_rows = key_cache[pages].reshape(-1, KVH, HD).astype(jnp.float32)
    value_rows = value_cache[pages].reshape(-1, KVH, HD).astype(jnp.float32)
    grouped = query_row.reshape(KVH, QH // KVH, HD).astype(jnp.float32)
    scores = jnp.einsum('gqd,tgd->gqt', grouped, key_rows) * HD ** -0.5
    own_score = jnp.einsum('gqd,gd->gq', grouped, key_new.reshape(KVH, HD).astype(jnp.float32)) * HD ** -0.5
    live_mask = (jnp.arange(key_rows.shape[0]).astype(jnp.int32) < length)[None, None, :]
    top_score = jnp.maximum(jnp.max(jnp.where(live_mask, scores, -1e30), axis=2), own_score)
    exp_terms = jnp.where(live_mask, jnp.exp(scores - top_score[:, :, None]), 0.0)
    own_exp = jnp.exp(own_score - top_score)
    total_mass = jnp.sum(exp_terms, axis=2) + own_exp
    weights = (exp_terms / total_mass[:, :, None]).astype(jnp.bfloat16)
    own_weight = (own_exp / total_mass).astype(jnp.bfloat16)
    summed = jnp.einsum('gqt,tgd->gqd', weights.astype(jnp.float32), value_rows)
    summed = summed + own_weight.astype(jnp.float32)[:, :, None] * value_new.reshape(KVH, 1, HD).astype(jnp.float32)
    return summed.reshape(-1).astype(jnp.bfloat16)


def reference(queries, new_key, new_value, key_cache, value_cache, lengths, page_table, residual, out_weight, gate_weight, up_weight, down_weight):
    owner_base = (jnp.arange(REQS).astype(jnp.int32) // REQ_DEV * POOL).astype(jnp.int32)
    pages = (page_table + owner_base[:, None]).astype(jnp.int32)

    def attend_request(request_item):
        return attend_each(request_item, key_cache, value_cache)

    attention = lax.map(attend_request, (queries, new_key, new_value, lengths, pages))
    mixed = (residual.astype(jnp.float32) + jnp.dot(attention, out_weight, preferred_element_type=jnp.float32)).astype(jnp.bfloat16)
    gate_acts = jnp.dot(mixed, gate_weight, preferred_element_type=jnp.float32)
    up_acts = jnp.dot(mixed, up_weight, preferred_element_type=jnp.float32)
    hidden = (jax.nn.silu(gate_acts) * up_acts).astype(jnp.bfloat16)
    down_part = jnp.dot(hidden, down_weight, preferred_element_type=jnp.float32)
    return (mixed.astype(jnp.float32) + down_part).astype(jnp.bfloat16)
```

```python
import jax
import jax.numpy as jnp
from jax import lax
from jax.sharding import PartitionSpec as P

HD = 128


def attend_pool(queries, new_key, new_value, key_pool, value_pool, lengths, page_table):
    row_count = queries.shape[0]
    pool_pages, page_rows, kv_width = key_pool.shape
    groups = kv_width // HD
    per_group = queries.shape[1] // kv_width
    pages_max = page_table.shape[1]
    pool_len = pool_pages * page_rows

    slot_start = lax.broadcasted_iota(jnp.int32, (row_count, pages_max), 1) * page_rows
    slot_live = slot_start < lengths[:, None]
    match = (page_table[:, :, None] == lax.broadcasted_iota(jnp.int32, (1, 1, pool_pages), 2)) & slot_live[
        :, :, None
    ]
    owned = jnp.any(match, axis=1)
    base = jnp.sum(jnp.where(match, slot_start[:, :, None], 0), axis=1)
    position = base[:, :, None] + lax.broadcasted_iota(jnp.int32, (1, 1, page_rows), 2)
    live_mask = (owned[:, :, None] & (position < lengths[:, None, None])).reshape(row_count, pool_len)
    live_mask = live_mask[:, None, None, :]

    key_rows = key_pool.reshape(pool_len, groups, HD)
    value_rows = value_pool.reshape(pool_len, groups, HD)
    grouped = queries.reshape(row_count, groups, per_group, HD)
    scores = jnp.einsum(
        "rgqd,tgd->rgqt", grouped, key_rows, preferred_element_type=jnp.float32
    ) * HD ** (-0.5)
    own_score = jnp.einsum(
        "rgqd,rgd->rgq",
        grouped,
        new_key.reshape(row_count, groups, HD),
        preferred_element_type=jnp.float32,
    ) * HD ** (-0.5)
    top_score = jnp.maximum(jnp.max(jnp.where(live_mask, scores, -1e30), axis=3), own_score)
    exp_terms = jnp.where(live_mask, jnp.exp(scores - top_score[..., None]), 0.0)
    own_exp = jnp.exp(own_score - top_score)
    total_mass = jnp.sum(exp_terms, axis=3) + own_exp
    weights = (exp_terms / total_mass[..., None]).astype(jnp.bfloat16)
    own_weight = (own_exp / total_mass).astype(jnp.bfloat16)
    summed = jnp.einsum("rgqt,tgd->rgqd", weights, value_rows, preferred_element_type=jnp.float32)
    summed = summed + own_weight.astype(jnp.float32)[..., None] * new_value.reshape(
        row_count, groups, 1, HD
    ).astype(jnp.float32)
    return summed.reshape(row_count, -1).astype(jnp.bfloat16)


def body(
    queries,
    new_key,
    new_value,
    key_cache,
    value_cache,
    lengths,
    page_table,
    residual,
    out_weight,
    gate_weight,
    up_weight,
    down_weight,
):
    n_req = lax.axis_size("req")
    head = lax.axis_index("head")
    swap = [(0, 1), (1, 0)]
    half = out_weight.shape[0] // 2
    cols = out_weight.shape[1]

    partner_rows = lax.dynamic_slice_in_dim(out_weight, (1 - head) * half, half, axis=0)
    lent_rows = lax.ppermute(partner_rows, "head", swap)
    own_rows = lax.dynamic_slice_in_dim(out_weight, head * half, half, axis=0)

    attention = attend_pool(
        queries, new_key, new_value, key_cache, value_cache, lengths, page_table
    )
    features = lax.all_gather(attention, "req", axis=0, tiled=True)
    both = jnp.dot(
        features,
        jnp.concatenate([own_rows, lent_rows], axis=1),
        preferred_element_type=jnp.float32,
    )
    attn_update = both[:, :cols] + lax.ppermute(both[:, cols:], "head", swap)
    mixed_rows = (residual.astype(jnp.float32) + attn_update).astype(jnp.bfloat16)
    shard_piece = lax.all_gather(mixed_rows, "req", axis=1, tiled=True)
    gate_acts = jnp.dot(shard_piece, gate_weight, preferred_element_type=jnp.float32)
    up_acts = jnp.dot(shard_piece, up_weight, preferred_element_type=jnp.float32)
    gate_full, up_full = lax.psum((gate_acts, up_acts), "head")
    hidden = (jax.nn.silu(gate_full) * up_full).astype(jnp.bfloat16)
    down_acts = jnp.dot(hidden, down_weight, preferred_element_type=jnp.float32)
    tokens = down_acts.shape[0]
    pieces = (
        down_acts.astype(jnp.bfloat16)
        .reshape(tokens, n_req, down_acts.shape[1] // n_req)
        .transpose(1, 0, 2)
    )
    gathered = lax.all_to_all(pieces, "req", 0, 0, tiled=True)
    down_part = jnp.sum(gathered.astype(jnp.float32), axis=0)
    return (mixed_rows.astype(jnp.float32) + down_part).astype(jnp.bfloat16)


def solution(mesh):
    return jax.shard_map(
        body,
        mesh=mesh,
        in_specs=(
            P("req", "head"),
            P("req", "head"),
            P("req", "head"),
            P("req", None, "head"),
            P("req", None, "head"),
            P("req"),
            P("req", None),
            P(None, ("head", "req")),
            P(None, ("head", "req")),
            P("head", "req"),
            P("head", "req"),
            P("req", "head"),
        ),
        out_specs=P(None, ("head", "req")),
        check_vma=False,
    )
```

```python
import jax
import jax.numpy as jnp
from jax import lax
from jax.sharding import PartitionSpec as P

HD = 128


def attend_pool(queries, new_key, new_value, key_pool, value_pool, lengths, page_table):
    row_count = queries.shape[0]
    pool_pages, page_rows, kv_width = key_pool.shape
    groups = kv_width // HD
    per_group = queries.shape[1] // kv_width
    pages_max = page_table.shape[1]
    pool_len = pool_pages * page_rows

    slot_start = lax.broadcasted_iota(jnp.int32, (row_count, pages_max), 1) * page_rows
    slot_live = slot_start < lengths[:, None]
    match = (page_table[:, :, None] == lax.broadcasted_iota(jnp.int32, (1, 1, pool_pages), 2)) & slot_live[
        :, :, None
    ]
    owned = jnp.any(match, axis=1)
    base = jnp.sum(jnp.where(match, slot_start[:, :, None], 0), axis=1)
    position = base[:, :, None] + lax.broadcasted_iota(jnp.int32, (1, 1, page_rows), 2)
    live_mask = (owned[:, :, None] & (position < lengths[:, None, None])).reshape(row_count, pool_len)
    live_mask = live_mask[:, None, None, :]

    key_rows = key_pool.reshape(pool_len, groups, HD)
    value_rows = value_pool.reshape(pool_len, groups, HD)
    grouped = queries.reshape(row_count, groups, per_group, HD)
    scores = jnp.einsum(
        "rgqd,tgd->rgqt", grouped, key_rows, preferred_element_type=jnp.float32
    ) * HD ** (-0.5)
    own_score = jnp.einsum(
        "rgqd,rgd->rgq",
        grouped,
        new_key.reshape(row_count, groups, HD),
        preferred_element_type=jnp.float32,
    ) * HD ** (-0.5)
    top_score = jnp.maximum(jnp.max(jnp.where(live_mask, scores, -1e30), axis=3), own_score)
    exp_terms = jnp.where(live_mask, jnp.exp(scores - top_score[..., None]), 0.0)
    own_exp = jnp.exp(own_score - top_score)
    total_mass = jnp.sum(exp_terms, axis=3) + own_exp
    weights = (exp_terms / total_mass[..., None]).astype(jnp.bfloat16)
    own_weight = (own_exp / total_mass).astype(jnp.bfloat16)
    summed = jnp.einsum("rgqt,tgd->rgqd", weights, value_rows, preferred_element_type=jnp.float32)
    summed = summed + own_weight.astype(jnp.float32)[..., None] * new_value.reshape(
        row_count, groups, 1, HD
    ).astype(jnp.float32)
    return summed.reshape(row_count, -1).astype(jnp.bfloat16)


def gather_rows(block, n_req):
    copies = jnp.broadcast_to(block[None], (n_req,) + block.shape)
    gathered = lax.all_to_all(copies, "req", 0, 0, tiled=True)
    return gathered.reshape(n_req * block.shape[0], *block.shape[1:])


def body(
    queries,
    new_key,
    new_value,
    key_cache,
    value_cache,
    lengths,
    page_table,
    residual,
    out_weight,
    gate_weight,
    up_weight,
    down_weight,
):
    n_req = lax.axis_size("req")
    head = lax.axis_index("head")
    swap = [(0, 1), (1, 0)]
    half = out_weight.shape[0] // 2
    cols = out_weight.shape[1]

    partner_rows = lax.dynamic_slice_in_dim(out_weight, (1 - head) * half, half, axis=0)
    lent_rows = lax.ppermute(partner_rows, "head", swap)
    own_rows = lax.dynamic_slice_in_dim(out_weight, head * half, half, axis=0)

    attention = attend_pool(
        queries, new_key, new_value, key_cache, value_cache, lengths, page_table
    )
    features = gather_rows(attention, n_req)
    both = jnp.dot(
        features,
        jnp.concatenate([own_rows, lent_rows], axis=1),
        preferred_element_type=jnp.float32,
    )
    attn_update = both[:, :cols] + lax.ppermute(both[:, cols:], "head", swap)
    mixed_rows = (residual.astype(jnp.float32) + attn_update).astype(jnp.bfloat16)
    shard_piece = gather_rows(mixed_rows.T, n_req).reshape(n_req, *mixed_rows.T.shape)
    shard_piece = shard_piece.transpose(2, 0, 1).reshape(mixed_rows.shape[0], -1)
    gate_acts = jnp.dot(shard_piece, gate_weight, preferred_element_type=jnp.float32)
    up_acts = jnp.dot(shard_piece, up_weight, preferred_element_type=jnp.float32)
    acts = jnp.concatenate([gate_acts, up_acts], axis=1)
    acts = acts + lax.ppermute(acts, "head", swap)
    gate_full, up_full = jnp.split(acts, 2, axis=1)
    hidden = (jax.nn.silu(gate_full) * up_full).astype(jnp.bfloat16)
    down_acts = jnp.dot(hidden, down_weight, preferred_element_type=jnp.float32)
    tokens = down_acts.shape[0]
    pieces = (
        down_acts.astype(jnp.bfloat16)
        .reshape(tokens, n_req, down_acts.shape[1] // n_req)
        .transpose(1, 0, 2)
    )
    gathered = lax.all_to_all(pieces, "req", 0, 0, tiled=True)
    down_part = jnp.sum(gathered.astype(jnp.float32), axis=0)
    return (mixed_rows.astype(jnp.float32) + down_part).astype(jnp.bfloat16)


def solution(mesh):
    return jax.shard_map(
        body,
        mesh=mesh,
        in_specs=(
            P("req", "head"),
            P("req", "head"),
            P("req", "head"),
            P("req", None, "head"),
            P("req", None, "head"),
            P("req"),
            P("req", None),
            P(None, ("head", "req")),
            P(None, ("head", "req")),
            P("head", "req"),
            P("head", "req"),
            P("req", "head"),
        ),
        out_specs=P(None, ("head", "req")),
        check_vma=False,
    )
```

```python
import jax
import jax.numpy as jnp
from jax import lax
from jax.sharding import PartitionSpec as P

HD = 128


def attend_pool(queries, new_key, new_value, key_pool, value_pool, lengths, page_table):
    row_count = queries.shape[0]
    pool_pages, page_rows, kv_width = key_pool.shape
    groups = kv_width // HD
    per_group = queries.shape[1] // kv_width
    pages_max = page_table.shape[1]
    pool_len = pool_pages * page_rows

    slot_start = lax.broadcasted_iota(jnp.int32, (row_count, pages_max), 1) * page_rows
    slot_live = slot_start < lengths[:, None]
    match = (page_table[:, :, None] == lax.broadcasted_iota(jnp.int32, (1, 1, pool_pages), 2)) & slot_live[
        :, :, None
    ]
    owned = jnp.any(match, axis=1)
    base = jnp.sum(jnp.where(match, slot_start[:, :, None], 0), axis=1)
    position = base[:, :, None] + lax.broadcasted_iota(jnp.int32, (1, 1, page_rows), 2)
    live_mask = (owned[:, :, None] & (position < lengths[:, None, None])).reshape(row_count, pool_len)
    live_mask = live_mask[:, None, None, :]

    key_rows = key_pool.reshape(pool_len, kv_width)
    value_rows = value_pool.reshape(pool_len, kv_width)
    grouped = queries.reshape(row_count, groups, per_group, HD)
    group_eye = jnp.eye(groups, dtype=queries.dtype)
    spread = (grouped[:, :, :, None, :] * group_eye[None, :, None, :, None]).reshape(
        row_count * groups * per_group, kv_width
    )
    scores = lax.dot_general(
        spread, key_rows, (((1,), (1,)), ((), ())), preferred_element_type=jnp.float32
    ).reshape(row_count, groups, per_group, pool_len) * HD ** (-0.5)
    own_score = jnp.einsum(
        "rgqd,rgd->rgq",
        grouped,
        new_key.reshape(row_count, groups, HD),
        preferred_element_type=jnp.float32,
    ) * HD ** (-0.5)
    top_score = jnp.maximum(jnp.max(jnp.where(live_mask, scores, -1e30), axis=3), own_score)
    exp_terms = jnp.where(live_mask, jnp.exp(scores - top_score[..., None]), 0.0)
    own_exp = jnp.exp(own_score - top_score)
    total_mass = jnp.sum(exp_terms, axis=3) + own_exp
    weights = (exp_terms / total_mass[..., None]).astype(jnp.bfloat16)
    own_weight = (own_exp / total_mass).astype(jnp.bfloat16)
    every = jnp.dot(
        weights.reshape(row_count * groups * per_group, pool_len),
        value_rows,
        preferred_element_type=jnp.float32,
    ).reshape(row_count, groups, per_group, groups, HD)
    summed = jnp.sum(
        every * group_eye.astype(jnp.float32)[None, :, None, :, None], axis=3
    )
    summed = summed + own_weight.astype(jnp.float32)[..., None] * new_value.reshape(
        row_count, groups, 1, HD
    ).astype(jnp.float32)
    return summed.reshape(row_count, -1).astype(jnp.bfloat16)


def gather_rows(block, n_req):
    copies = jnp.broadcast_to(block[None], (n_req,) + block.shape)
    gathered = lax.all_to_all(copies, "req", 0, 0, tiled=True)
    return gathered.reshape(n_req * block.shape[0], *block.shape[1:])


def body(
    queries,
    new_key,
    new_value,
    key_cache,
    value_cache,
    lengths,
    page_table,
    residual,
    out_weight,
    gate_weight,
    up_weight,
    down_weight,
):
    n_req = lax.axis_size("req")
    head = lax.axis_index("head")
    swap = [(0, 1), (1, 0)]
    half = out_weight.shape[0] // 2
    cols = out_weight.shape[1]

    partner_rows = lax.dynamic_slice_in_dim(out_weight, (1 - head) * half, half, axis=0)
    lent_rows = lax.ppermute(partner_rows, "head", swap)
    own_rows = lax.dynamic_slice_in_dim(out_weight, head * half, half, axis=0)

    attention = attend_pool(
        queries, new_key, new_value, key_cache, value_cache, lengths, page_table
    )
    features = gather_rows(attention, n_req)
    both = jnp.dot(
        features,
        jnp.concatenate([own_rows, lent_rows], axis=1),
        preferred_element_type=jnp.float32,
    )
    attn_update = both[:, :cols] + lax.ppermute(both[:, cols:], "head", swap)
    mixed_rows = (residual.astype(jnp.float32) + attn_update).astype(jnp.bfloat16)
    shard_piece = gather_rows(mixed_rows.T, n_req).reshape(n_req, *mixed_rows.T.shape)
    shard_piece = shard_piece.transpose(2, 0, 1).reshape(mixed_rows.shape[0], -1)
    gate_acts = jnp.dot(shard_piece, gate_weight, preferred_element_type=jnp.float32)
    up_acts = jnp.dot(shard_piece, up_weight, preferred_element_type=jnp.float32)
    acts = jnp.concatenate([gate_acts, up_acts], axis=1)
    acts = acts + lax.ppermute(acts, "head", swap)
    gate_full, up_full = jnp.split(acts, 2, axis=1)
    hidden = (jax.nn.silu(gate_full) * up_full).astype(jnp.bfloat16)
    pieces = jnp.einsum(
        "tf,fnc->ntc",
        hidden,
        down_weight.reshape(down_weight.shape[0], n_req, down_weight.shape[1] // n_req),
        preferred_element_type=jnp.float32,
    ).astype(jnp.bfloat16)
    gathered = lax.all_to_all(pieces, "req", 0, 0, tiled=True)
    down_part = jnp.sum(gathered.astype(jnp.float32), axis=0)
    return (mixed_rows.astype(jnp.float32) + down_part).astype(jnp.bfloat16)


def solution(mesh):
    return jax.shard_map(
        body,
        mesh=mesh,
        in_specs=(
            P("req", "head"),
            P("req", "head"),
            P("req", "head"),
            P("req", None, "head"),
            P("req", None, "head"),
            P("req"),
            P("req", None),
            P(None, ("head", "req")),
            P(None, ("head", "req")),
            P("head", "req"),
            P("head", "req"),
            P("req", "head"),
        ),
        out_specs=P(None, ("head", "req")),
        check_vma=False,
    )
```

```python
import jax
import jax.numpy as jnp
from jax import lax
from jax.experimental import pallas as pl
from jax.experimental.pallas import tpu as pltpu
from jax.sharding import PartitionSpec as P

HD = 128
INTERPRET = False


def softmax_kernel(q_ref, k_ref, v_ref, live_ref, own_ref, out_ref, own_w_ref, w_scr):
    rows_per_req = q_ref.shape[0] // live_ref.shape[0]
    scores = lax.dot_general(
        q_ref[...], k_ref[...], (((1,), (1,)), ((), ())), preferred_element_type=jnp.float32
    ) * HD ** (-0.5)
    for r in range(live_ref.shape[0]):
        rows = slice(r * rows_per_req, (r + 1) * rows_per_req)
        part = scores[rows, :]
        live = live_ref[r : r + 1, :] != 0
        own = own_ref[rows, :]
        top = jnp.maximum(jnp.max(jnp.where(live, part, -1e30), axis=1, keepdims=True), own)
        exp_terms = jnp.where(live, jnp.exp(part - top), 0.0)
        own_exp = jnp.exp(own - top)
        total = jnp.sum(exp_terms, axis=1, keepdims=True) + own_exp
        w_scr[rows, :] = (exp_terms / total).astype(jnp.bfloat16)
        own_w_ref[rows, :] = (own_exp / total).astype(jnp.bfloat16).astype(jnp.float32)
    out_ref[...] = jnp.dot(w_scr[...], v_ref[...], preferred_element_type=jnp.float32)


def attend_pool(queries, new_key, new_value, key_pool, value_pool, lengths, page_table):
    row_count = queries.shape[0]
    pool_pages, page_rows, kv_width = key_pool.shape
    groups = kv_width // HD
    per_group = queries.shape[1] // kv_width
    pages_max = page_table.shape[1]
    pool_len = pool_pages * page_rows

    slot_start = lax.broadcasted_iota(jnp.int32, (row_count, pages_max), 1) * page_rows
    slot_live = slot_start < lengths[:, None]
    match = (page_table[:, :, None] == lax.broadcasted_iota(jnp.int32, (1, 1, pool_pages), 2)) & slot_live[
        :, :, None
    ]
    owned = jnp.any(match, axis=1)
    base = jnp.sum(jnp.where(match, slot_start[:, :, None], 0), axis=1)
    position = base[:, :, None] + lax.broadcasted_iota(jnp.int32, (1, 1, page_rows), 2)
    live_mask = (owned[:, :, None] & (position < lengths[:, None, None])).reshape(row_count, pool_len)

    key_rows = key_pool.reshape(pool_len, kv_width)
    value_rows = value_pool.reshape(pool_len, kv_width)
    grouped = queries.reshape(row_count, groups, per_group, HD)
    group_eye = jnp.eye(groups, dtype=queries.dtype)
    spread = (grouped[:, :, :, None, :] * group_eye[None, :, None, :, None]).reshape(
        row_count * groups * per_group, kv_width
    )
    own_score = jnp.einsum(
        "rgqd,rgd->rgq",
        grouped,
        new_key.reshape(row_count, groups, HD),
        preferred_element_type=jnp.float32,
    ) * HD ** (-0.5)
    n_rows = row_count * groups * per_group
    vmem = pl.BlockSpec(memory_space=pltpu.VMEM)
    flat, own_w = pl.pallas_call(
        softmax_kernel,
        out_shape=(
            jax.ShapeDtypeStruct((n_rows, kv_width), jnp.float32),
            jax.ShapeDtypeStruct((n_rows, 1), jnp.float32),
        ),
        in_specs=[vmem] * 5,
        out_specs=(vmem, vmem),
        scratch_shapes=[pltpu.VMEM((n_rows, pool_len), jnp.bfloat16)],
        interpret=INTERPRET,
    )(spread, key_rows, value_rows, live_mask.astype(jnp.int32), own_score.reshape(n_rows, 1))
    every = flat.reshape(row_count, groups, per_group, groups, HD)
    own_weight = own_w.reshape(row_count, groups, per_group)
    summed = jnp.sum(
        every * group_eye.astype(jnp.float32)[None, :, None, :, None], axis=3
    )
    summed = summed + own_weight[..., None] * new_value.reshape(
        row_count, groups, 1, HD
    ).astype(jnp.float32)
    return summed.reshape(row_count, -1).astype(jnp.bfloat16)


def gather_rows(block, n_req):
    copies = jnp.broadcast_to(block[None], (n_req,) + block.shape)
    gathered = lax.all_to_all(copies, "req", 0, 0, tiled=True)
    return gathered.reshape(n_req * block.shape[0], *block.shape[1:])


def body(
    queries,
    new_key,
    new_value,
    key_cache,
    value_cache,
    lengths,
    page_table,
    residual,
    out_weight,
    gate_weight,
    up_weight,
    down_weight,
):
    n_req = lax.axis_size("req")
    head = lax.axis_index("head")
    swap = [(0, 1), (1, 0)]
    half = out_weight.shape[0] // 2
    cols = out_weight.shape[1]

    partner_rows = lax.dynamic_slice_in_dim(out_weight, (1 - head) * half, half, axis=0)
    lent_rows = lax.ppermute(partner_rows, "head", swap)
    own_rows = lax.dynamic_slice_in_dim(out_weight, head * half, half, axis=0)

    attention = attend_pool(
        queries, new_key, new_value, key_cache, value_cache, lengths, page_table
    )
    features = gather_rows(attention, n_req)
    both = jnp.dot(
        features,
        jnp.concatenate([own_rows, lent_rows], axis=1),
        preferred_element_type=jnp.float32,
    )
    attn_update = both[:, :cols] + lax.ppermute(both[:, cols:], "head", swap)
    mixed_rows = (residual.astype(jnp.float32) + attn_update).astype(jnp.bfloat16)
    shard_piece = gather_rows(mixed_rows.T, n_req).reshape(n_req, *mixed_rows.T.shape)
    shard_piece = shard_piece.transpose(2, 0, 1).reshape(mixed_rows.shape[0], -1)
    gate_acts = jnp.dot(shard_piece, gate_weight, preferred_element_type=jnp.float32)
    up_acts = jnp.dot(shard_piece, up_weight, preferred_element_type=jnp.float32)
    acts = jnp.concatenate([gate_acts, up_acts], axis=1)
    acts = acts + lax.ppermute(acts, "head", swap)
    gate_full, up_full = jnp.split(acts, 2, axis=1)
    hidden = (jax.nn.silu(gate_full) * up_full).astype(jnp.bfloat16)
    pieces = jnp.einsum(
        "tf,fnc->ntc",
        hidden,
        down_weight.reshape(down_weight.shape[0], n_req, down_weight.shape[1] // n_req),
        preferred_element_type=jnp.float32,
    ).astype(jnp.bfloat16)
    gathered = lax.all_to_all(pieces, "req", 0, 0, tiled=True)
    down_part = jnp.sum(gathered.astype(jnp.float32), axis=0)
    return (mixed_rows.astype(jnp.float32) + down_part).astype(jnp.bfloat16)


def solution(mesh):
    return jax.shard_map(
        body,
        mesh=mesh,
        in_specs=(
            P("req", "head"),
            P("req", "head"),
            P("req", "head"),
            P("req", None, "head"),
            P("req", None, "head"),
            P("req"),
            P("req", None),
            P(None, ("head", "req")),
            P(None, ("head", "req")),
            P("head", "req"),
            P("head", "req"),
            P("req", "head"),
        ),
        out_specs=P(None, ("head", "req")),
        check_vma=False,
    )
```

```python
import jax
import jax.numpy as jnp
from jax import lax
from jax.experimental import pallas as pl
from jax.experimental.pallas import tpu as pltpu
from jax.sharding import PartitionSpec as P

HD = 128
INTERPRET = False


def softmax_kernel(q_ref, k_ref, v_ref, live_ref, own_ref, out_ref, own_w_ref, w_scr):
    groups, rows, _ = q_ref.shape
    requests = live_ref.shape[0]
    per_req = rows // requests
    for g in range(groups):
        cols = slice(g * HD, (g + 1) * HD)
        scores = lax.dot_general(
            q_ref[g], k_ref[:, cols], (((1,), (1,)), ((), ())), preferred_element_type=jnp.float32
        ) * HD ** (-0.5)
        for r in range(requests):
            part_rows = slice(r * per_req, (r + 1) * per_req)
            part = scores[part_rows, :]
            live = live_ref[r : r + 1, :] != 0
            own = own_ref[g, part_rows, :]
            top = jnp.maximum(jnp.max(jnp.where(live, part, -1e30), axis=1, keepdims=True), own)
            exp_terms = jnp.where(live, jnp.exp(part - top), 0.0)
            own_exp = jnp.exp(own - top)
            total = jnp.sum(exp_terms, axis=1, keepdims=True) + own_exp
            w_scr[part_rows, :] = (exp_terms / total).astype(jnp.bfloat16)
            own_w_ref[g, part_rows, :] = (own_exp / total).astype(jnp.bfloat16).astype(jnp.float32)
        out_ref[g] = jnp.dot(w_scr[...], v_ref[:, cols], preferred_element_type=jnp.float32)


def attend_pool(queries, new_key, new_value, key_pool, value_pool, lengths, page_table):
    row_count = queries.shape[0]
    pool_pages, page_rows, kv_width = key_pool.shape
    groups = kv_width // HD
    per_group = queries.shape[1] // kv_width
    pages_max = page_table.shape[1]
    pool_len = pool_pages * page_rows

    slot_start = lax.broadcasted_iota(jnp.int32, (row_count, pages_max), 1) * page_rows
    slot_live = slot_start < lengths[:, None]
    match = (page_table[:, :, None] == lax.broadcasted_iota(jnp.int32, (1, 1, pool_pages), 2)) & slot_live[
        :, :, None
    ]
    owned = jnp.any(match, axis=1)
    base = jnp.sum(jnp.where(match, slot_start[:, :, None], 0), axis=1)
    position = base[:, :, None] + lax.broadcasted_iota(jnp.int32, (1, 1, page_rows), 2)
    live_mask = (owned[:, :, None] & (position < lengths[:, None, None])).reshape(row_count, pool_len)

    key_rows = key_pool.reshape(pool_len, kv_width)
    value_rows = value_pool.reshape(pool_len, kv_width)
    grouped = queries.reshape(row_count, groups, per_group, HD)
    own_score = jnp.einsum(
        "rgqd,rgd->grq",
        grouped,
        new_key.reshape(row_count, groups, HD),
        preferred_element_type=jnp.float32,
    ) * HD ** (-0.5)
    by_group = grouped.transpose(1, 0, 2, 3).reshape(groups, row_count * per_group, HD)
    vmem = pl.BlockSpec(memory_space=pltpu.VMEM)
    summed, own_w = pl.pallas_call(
        softmax_kernel,
        out_shape=(
            jax.ShapeDtypeStruct((groups, row_count * per_group, HD), jnp.float32),
            jax.ShapeDtypeStruct((groups, row_count * per_group, 1), jnp.float32),
        ),
        in_specs=[vmem] * 5,
        out_specs=(vmem, vmem),
        scratch_shapes=[pltpu.VMEM((row_count * per_group, pool_len), jnp.bfloat16)],
        interpret=INTERPRET,
    )(
        by_group,
        key_rows,
        value_rows,
        live_mask.astype(jnp.int32),
        own_score.reshape(groups, row_count * per_group, 1),
    )
    summed = summed.reshape(groups, row_count, per_group, HD).transpose(1, 0, 2, 3)
    own_weight = own_w.reshape(groups, row_count, per_group).transpose(1, 0, 2)
    summed = summed + own_weight[..., None] * new_value.reshape(
        row_count, groups, 1, HD
    ).astype(jnp.float32)
    return summed.reshape(row_count, -1).astype(jnp.bfloat16)


def gather_rows(block, n_req):
    copies = jnp.broadcast_to(block[None], (n_req,) + block.shape)
    gathered = lax.all_to_all(copies, "req", 0, 0, tiled=True)
    return gathered.reshape(n_req * block.shape[0], *block.shape[1:])


def body(
    queries,
    new_key,
    new_value,
    key_cache,
    value_cache,
    lengths,
    page_table,
    residual,
    out_weight,
    gate_weight,
    up_weight,
    down_weight,
):
    n_req = lax.axis_size("req")
    head = lax.axis_index("head")
    swap = [(0, 1), (1, 0)]
    half = out_weight.shape[0] // 2
    cols = out_weight.shape[1]

    partner_rows = lax.dynamic_slice_in_dim(out_weight, (1 - head) * half, half, axis=0)
    lent_rows = lax.ppermute(partner_rows, "head", swap)
    own_rows = lax.dynamic_slice_in_dim(out_weight, head * half, half, axis=0)

    attention = attend_pool(
        queries, new_key, new_value, key_cache, value_cache, lengths, page_table
    )
    features = gather_rows(attention, n_req)
    both = jnp.dot(
        features,
        jnp.concatenate([own_rows, lent_rows], axis=1),
        preferred_element_type=jnp.float32,
    )
    attn_update = both[:, :cols] + lax.ppermute(both[:, cols:], "head", swap)
    mixed_rows = (residual.astype(jnp.float32) + attn_update).astype(jnp.bfloat16)
    shard_piece = gather_rows(mixed_rows.T, n_req).reshape(n_req, *mixed_rows.T.shape)
    shard_piece = shard_piece.transpose(2, 0, 1).reshape(mixed_rows.shape[0], -1)
    gate_acts = jnp.dot(shard_piece, gate_weight, preferred_element_type=jnp.float32)
    up_acts = jnp.dot(shard_piece, up_weight, preferred_element_type=jnp.float32)
    units = gate_acts.shape[1] // 2
    gate_parts = gate_acts.reshape(gate_acts.shape[0], 2, units)
    up_parts = up_acts.reshape(up_acts.shape[0], 2, units)
    own_part = jnp.concatenate(
        [jnp.take(gate_parts, head, axis=1), jnp.take(up_parts, head, axis=1)], axis=1
    )
    lent_part = jnp.concatenate(
        [jnp.take(gate_parts, 1 - head, axis=1), jnp.take(up_parts, 1 - head, axis=1)], axis=1
    )
    acts = own_part + lax.ppermute(lent_part, "head", swap)
    gate_half, up_half = jnp.split(acts, 2, axis=1)
    hidden_half = (jax.nn.silu(gate_half) * up_half).astype(jnp.bfloat16)
    other_half = lax.ppermute(hidden_half, "head", swap)
    halves = jnp.where(head == 0, jnp.stack([hidden_half, other_half]), jnp.stack([other_half, hidden_half]))
    hidden = halves.transpose(1, 0, 2).reshape(hidden_half.shape[0], -1)
    pieces = jnp.einsum(
        "tf,fnc->ntc",
        hidden,
        down_weight.reshape(down_weight.shape[0], n_req, down_weight.shape[1] // n_req),
        preferred_element_type=jnp.float32,
    ).astype(jnp.bfloat16)
    gathered = lax.all_to_all(pieces, "req", 0, 0, tiled=True)
    down_part = jnp.sum(gathered.astype(jnp.float32), axis=0)
    return (mixed_rows.astype(jnp.float32) + down_part).astype(jnp.bfloat16)


def solution(mesh):
    return jax.shard_map(
        body,
        mesh=mesh,
        in_specs=(
            P("req", "head"),
            P("req", "head"),
            P("req", "head"),
            P("req", None, "head"),
            P("req", None, "head"),
            P("req"),
            P("req", None),
            P(None, ("head", "req")),
            P(None, ("head", "req")),
            P("head", "req"),
            P("head", "req"),
            P("req", "head"),
        ),
        out_specs=P(None, ("head", "req")),
        check_vma=False,
    )
```

```python
import jax
import jax.numpy as jnp
from jax import lax
from jax.experimental import pallas as pl
from jax.experimental.pallas import tpu as pltpu
from jax.sharding import PartitionSpec as P

HD = 128
INTERPRET = False


def softmax_kernel(q_ref, k_ref, v_ref, live_ref, own_ref, out_ref, own_w_ref, w_scr):
    rows = q_ref.shape[1]
    requests = live_ref.shape[0]
    per_req = rows // requests
    scores = lax.dot_general(
        q_ref[0], k_ref[...], (((1,), (1,)), ((), ())), preferred_element_type=jnp.float32
    ) * HD ** (-0.5)
    for r in range(requests):
        part_rows = slice(r * per_req, (r + 1) * per_req)
        part = scores[part_rows, :]
        live = live_ref[r : r + 1, :] != 0
        own = own_ref[0, part_rows, :]
        top = jnp.maximum(jnp.max(jnp.where(live, part, -1e30), axis=1, keepdims=True), own)
        exp_terms = jnp.where(live, jnp.exp(part - top), 0.0)
        own_exp = jnp.exp(own - top)
        total = jnp.sum(exp_terms, axis=1, keepdims=True) + own_exp
        w_scr[part_rows, :] = (exp_terms / total).astype(jnp.bfloat16)
        own_w_ref[0, part_rows, :] = (own_exp / total).astype(jnp.bfloat16).astype(jnp.float32)
    out_ref[0] = jnp.dot(w_scr[...], v_ref[...], preferred_element_type=jnp.float32)


def attend_pool(queries, new_key, new_value, key_pool, value_pool, lengths, page_table):
    row_count = queries.shape[0]
    pool_pages, page_rows, kv_width = key_pool.shape
    groups = kv_width // HD
    per_group = queries.shape[1] // kv_width
    pages_max = page_table.shape[1]
    pool_len = pool_pages * page_rows

    slot_start = lax.broadcasted_iota(jnp.int32, (row_count, pages_max), 1) * page_rows
    slot_live = slot_start < lengths[:, None]
    match = (page_table[:, :, None] == lax.broadcasted_iota(jnp.int32, (1, 1, pool_pages), 2)) & slot_live[
        :, :, None
    ]
    owned = jnp.any(match, axis=1)
    base = jnp.sum(jnp.where(match, slot_start[:, :, None], 0), axis=1)
    position = base[:, :, None] + lax.broadcasted_iota(jnp.int32, (1, 1, page_rows), 2)
    live_mask = (owned[:, :, None] & (position < lengths[:, None, None])).reshape(row_count, pool_len)

    key_rows = key_pool.reshape(pool_len, kv_width)
    value_rows = value_pool.reshape(pool_len, kv_width)
    grouped = queries.reshape(row_count, groups, per_group, HD)
    own_score = jnp.einsum(
        "rgqd,rgd->grq",
        grouped,
        new_key.reshape(row_count, groups, HD),
        preferred_element_type=jnp.float32,
    ) * HD ** (-0.5)
    by_group = grouped.transpose(1, 0, 2, 3).reshape(groups, row_count * per_group, HD)
    n_rows = row_count * per_group
    per_step = pl.BlockSpec((1, n_rows, HD), lambda g: (g, 0, 0))
    per_step_col = pl.BlockSpec((1, n_rows, 1), lambda g: (g, 0, 0))
    lane_slice = pl.BlockSpec((pool_len, HD), lambda g: (0, g))
    summed, own_w = pl.pallas_call(
        softmax_kernel,
        grid=(groups,),
        out_shape=(
            jax.ShapeDtypeStruct((groups, n_rows, HD), jnp.float32),
            jax.ShapeDtypeStruct((groups, n_rows, 1), jnp.float32),
        ),
        in_specs=[
            per_step,
            lane_slice,
            lane_slice,
            pl.BlockSpec((row_count, pool_len), lambda g: (0, 0)),
            per_step_col,
        ],
        out_specs=(per_step, per_step_col),
        scratch_shapes=[pltpu.VMEM((n_rows, pool_len), jnp.bfloat16)],
        interpret=INTERPRET,
    )(
        by_group,
        key_rows,
        value_rows,
        live_mask.astype(jnp.int32),
        own_score.reshape(groups, row_count * per_group, 1),
    )
    summed = summed.reshape(groups, row_count, per_group, HD).transpose(1, 0, 2, 3)
    own_weight = own_w.reshape(groups, row_count, per_group).transpose(1, 0, 2)
    summed = summed + own_weight[..., None] * new_value.reshape(
        row_count, groups, 1, HD
    ).astype(jnp.float32)
    return summed.reshape(row_count, -1).astype(jnp.bfloat16)


def gather_rows(block, n_req):
    copies = jnp.broadcast_to(block[None], (n_req,) + block.shape)
    gathered = lax.all_to_all(copies, "req", 0, 0, tiled=True)
    return gathered.reshape(n_req * block.shape[0], *block.shape[1:])


def body(
    queries,
    new_key,
    new_value,
    key_cache,
    value_cache,
    lengths,
    page_table,
    residual,
    out_weight,
    gate_weight,
    up_weight,
    down_weight,
):
    n_req = lax.axis_size("req")
    head = lax.axis_index("head")
    swap = [(0, 1), (1, 0)]
    half = out_weight.shape[0] // 2
    cols = out_weight.shape[1]

    partner_rows = lax.dynamic_slice_in_dim(out_weight, (1 - head) * half, half, axis=0)
    lent_rows = lax.ppermute(partner_rows, "head", swap)
    own_rows = lax.dynamic_slice_in_dim(out_weight, head * half, half, axis=0)

    attention = attend_pool(
        queries, new_key, new_value, key_cache, value_cache, lengths, page_table
    )
    features = gather_rows(attention, n_req)
    both = jnp.dot(
        features,
        jnp.concatenate([own_rows, lent_rows], axis=1),
        preferred_element_type=jnp.float32,
    )
    attn_update = both[:, :cols] + lax.ppermute(both[:, cols:], "head", swap)
    mixed_rows = (residual.astype(jnp.float32) + attn_update).astype(jnp.bfloat16)
    shard_piece = gather_rows(mixed_rows.T, n_req).reshape(n_req, *mixed_rows.T.shape)
    shard_piece = shard_piece.transpose(2, 0, 1).reshape(mixed_rows.shape[0], -1)
    gate_acts = jnp.dot(shard_piece, gate_weight, preferred_element_type=jnp.float32)
    up_acts = jnp.dot(shard_piece, up_weight, preferred_element_type=jnp.float32)
    acts = jnp.concatenate([gate_acts, up_acts], axis=1)
    acts = acts + lax.ppermute(acts, "head", swap)
    gate_full, up_full = jnp.split(acts, 2, axis=1)
    hidden = (jax.nn.silu(gate_full) * up_full).astype(jnp.bfloat16)
    pieces = jnp.einsum(
        "tf,fnc->ntc",
        hidden,
        down_weight.reshape(down_weight.shape[0], n_req, down_weight.shape[1] // n_req),
        preferred_element_type=jnp.float32,
    ).astype(jnp.bfloat16)
    gathered = lax.all_to_all(pieces, "req", 0, 0, tiled=True)
    down_part = jnp.sum(gathered.astype(jnp.float32), axis=0)
    return (mixed_rows.astype(jnp.float32) + down_part).astype(jnp.bfloat16)


def solution(mesh):
    return jax.shard_map(
        body,
        mesh=mesh,
        in_specs=(
            P("req", "head"),
            P("req", "head"),
            P("req", "head"),
            P("req", None, "head"),
            P("req", None, "head"),
            P("req"),
            P("req", None),
            P(None, ("head", "req")),
            P(None, ("head", "req")),
            P("head", "req"),
            P("head", "req"),
            P("req", "head"),
        ),
        out_specs=P(None, ("head", "req")),
        check_vma=False,
    )
```

```python
import jax
import jax.numpy as jnp
from jax import lax
from jax.experimental import pallas as pl
from jax.experimental.pallas import tpu as pltpu
from jax.sharding import PartitionSpec as P

HD = 128
INTERPRET = False


def softmax_kernel(q_ref, k_ref, v_ref, live_ref, nk_ref, nv_ref, out_ref, w_scr, own_scr):
    rows = q_ref.shape[1]
    requests = live_ref.shape[0]
    per_req = rows // requests
    q = q_ref[0]
    scores = lax.dot_general(
        q, k_ref[...], (((1,), (1,)), ((), ())), preferred_element_type=jnp.float32
    ) * HD ** (-0.5)
    own_all = lax.dot_general(
        q, nk_ref[...], (((1,), (1,)), ((), ())), preferred_element_type=jnp.float32
    ) * HD ** (-0.5)
    for r in range(requests):
        part_rows = slice(r * per_req, (r + 1) * per_req)
        part = scores[part_rows, :]
        live = live_ref[r : r + 1, :] != 0
        own = own_all[part_rows, r : r + 1]
        top = jnp.maximum(jnp.max(jnp.where(live, part, -1e30), axis=1, keepdims=True), own)
        exp_terms = jnp.where(live, jnp.exp(part - top), 0.0)
        own_exp = jnp.exp(own - top)
        total = jnp.sum(exp_terms, axis=1, keepdims=True) + own_exp
        w_scr[part_rows, :] = (exp_terms / total).astype(jnp.bfloat16)
        own_weight = (own_exp / total).astype(jnp.bfloat16).astype(jnp.float32)
        own_scr[part_rows, :] = own_weight * nv_ref[r : r + 1, :].astype(jnp.float32)
    summed = jnp.dot(w_scr[...], v_ref[...], preferred_element_type=jnp.float32) + own_scr[...]
    out_ref[0] = summed.astype(out_ref.dtype)


def attend_pool(queries, new_key, new_value, key_pool, value_pool, lengths, page_table):
    row_count = queries.shape[0]
    pool_pages, page_rows, kv_width = key_pool.shape
    groups = kv_width // HD
    per_group = queries.shape[1] // kv_width
    pages_max = page_table.shape[1]
    pool_len = pool_pages * page_rows

    slot_start = lax.broadcasted_iota(jnp.int32, (row_count, pages_max), 1) * page_rows
    slot_live = slot_start < lengths[:, None]
    match = (page_table[:, :, None] == lax.broadcasted_iota(jnp.int32, (1, 1, pool_pages), 2)) & slot_live[
        :, :, None
    ]
    owned = jnp.any(match, axis=1)
    base = jnp.sum(jnp.where(match, slot_start[:, :, None], 0), axis=1)
    position = base[:, :, None] + lax.broadcasted_iota(jnp.int32, (1, 1, page_rows), 2)
    live_mask = (owned[:, :, None] & (position < lengths[:, None, None])).reshape(row_count, pool_len)

    key_rows = key_pool.reshape(pool_len, kv_width)
    value_rows = value_pool.reshape(pool_len, kv_width)
    grouped = queries.reshape(row_count, groups, per_group, HD)
    by_group = grouped.transpose(1, 0, 2, 3).reshape(groups, row_count * per_group, HD)
    n_rows = row_count * per_group
    per_step = pl.BlockSpec((1, n_rows, HD), lambda g: (g, 0, 0))
    lane_slice = pl.BlockSpec((pool_len, HD), lambda g: (0, g))
    new_slice = pl.BlockSpec((row_count, HD), lambda g: (0, g))
    summed = pl.pallas_call(
        softmax_kernel,
        grid=(groups,),
        out_shape=jax.ShapeDtypeStruct((groups, n_rows, HD), jnp.bfloat16),
        in_specs=[
            per_step,
            lane_slice,
            lane_slice,
            pl.BlockSpec((row_count, pool_len), lambda g: (0, 0)),
            new_slice,
            new_slice,
        ],
        out_specs=per_step,
        scratch_shapes=[
            pltpu.VMEM((n_rows, pool_len), jnp.bfloat16),
            pltpu.VMEM((n_rows, HD), jnp.float32),
        ],
        interpret=INTERPRET,
    )(by_group, key_rows, value_rows, live_mask.astype(jnp.int32), new_key, new_value)
    summed = summed.reshape(groups, row_count, per_group, HD).transpose(1, 0, 2, 3)
    return summed.reshape(row_count, -1)


def gather_rows(block, n_req):
    copies = jnp.broadcast_to(block[None], (n_req,) + block.shape)
    gathered = lax.all_to_all(copies, "req", 0, 0, tiled=True)
    return gathered.reshape(n_req * block.shape[0], *block.shape[1:])


def body(
    queries,
    new_key,
    new_value,
    key_cache,
    value_cache,
    lengths,
    page_table,
    residual,
    out_weight,
    gate_weight,
    up_weight,
    down_weight,
):
    n_req = lax.axis_size("req")
    head = lax.axis_index("head")
    swap = [(0, 1), (1, 0)]
    half = out_weight.shape[0] // 2
    cols = out_weight.shape[1]

    partner_rows = lax.dynamic_slice_in_dim(out_weight, (1 - head) * half, half, axis=0)
    lent_rows = lax.ppermute(partner_rows, "head", swap)
    own_rows = lax.dynamic_slice_in_dim(out_weight, head * half, half, axis=0)

    attention = attend_pool(
        queries, new_key, new_value, key_cache, value_cache, lengths, page_table
    )
    features = gather_rows(attention, n_req)
    both = jnp.dot(
        features,
        jnp.concatenate([own_rows, lent_rows], axis=1),
        preferred_element_type=jnp.float32,
    )
    attn_update = both[:, :cols] + lax.ppermute(both[:, cols:], "head", swap)
    mixed_rows = (residual.astype(jnp.float32) + attn_update).astype(jnp.bfloat16)
    shard_piece = gather_rows(mixed_rows.T, n_req).reshape(n_req, *mixed_rows.T.shape)
    shard_piece = shard_piece.transpose(2, 0, 1).reshape(mixed_rows.shape[0], -1)
    gate_acts = jnp.dot(shard_piece, gate_weight, preferred_element_type=jnp.float32)
    up_acts = jnp.dot(shard_piece, up_weight, preferred_element_type=jnp.float32)
    acts = jnp.concatenate([gate_acts, up_acts], axis=1)
    acts = acts + lax.ppermute(acts, "head", swap)
    gate_full, up_full = jnp.split(acts, 2, axis=1)
    hidden = (jax.nn.silu(gate_full) * up_full).astype(jnp.bfloat16)
    pieces = jnp.einsum(
        "tf,fnc->ntc",
        hidden,
        down_weight.reshape(down_weight.shape[0], n_req, down_weight.shape[1] // n_req),
        preferred_element_type=jnp.float32,
    ).astype(jnp.bfloat16)
    gathered = lax.all_to_all(pieces, "req", 0, 0, tiled=True)
    down_part = jnp.sum(gathered.astype(jnp.float32), axis=0)
    return (mixed_rows.astype(jnp.float32) + down_part).astype(jnp.bfloat16)


def solution(mesh):
    return jax.shard_map(
        body,
        mesh=mesh,
        in_specs=(
            P("req", "head"),
            P("req", "head"),
            P("req", "head"),
            P("req", None, "head"),
            P("req", None, "head"),
            P("req"),
            P("req", None),
            P(None, ("head", "req")),
            P(None, ("head", "req")),
            P("head", "req"),
            P("head", "req"),
            P("req", "head"),
        ),
        out_specs=P(None, ("head", "req")),
        check_vma=False,
    )
```

```python
import jax
import jax.numpy as jnp
from jax import lax
from jax.experimental import pallas as pl
from jax.experimental.pallas import tpu as pltpu
from jax.sharding import PartitionSpec as P

HD = 128
INTERPRET = False


def softmax_kernel(q_ref, k_ref, v_ref, live_ref, nk_ref, nv_ref, out_ref, q_scr, w_scr, own_scr):
    rows = q_scr.shape[0]
    requests = live_ref.shape[0]
    per_req = rows // requests
    for r in range(requests):
        for h in range(per_req):
            q_scr[r * per_req + h : r * per_req + h + 1, :] = q_ref[r : r + 1, h * HD : (h + 1) * HD]
    q = q_scr[...]
    scores = lax.dot_general(
        q, k_ref[...], (((1,), (1,)), ((), ())), preferred_element_type=jnp.float32
    ) * HD ** (-0.5)
    own_all = lax.dot_general(
        q, nk_ref[...], (((1,), (1,)), ((), ())), preferred_element_type=jnp.float32
    ) * HD ** (-0.5)
    for r in range(requests):
        part_rows = slice(r * per_req, (r + 1) * per_req)
        part = scores[part_rows, :]
        live = live_ref[r : r + 1, :] != 0
        own = own_all[part_rows, r : r + 1]
        top = jnp.maximum(jnp.max(jnp.where(live, part, -1e30), axis=1, keepdims=True), own)
        exp_terms = jnp.where(live, jnp.exp(part - top), 0.0)
        own_exp = jnp.exp(own - top)
        total = jnp.sum(exp_terms, axis=1, keepdims=True) + own_exp
        w_scr[part_rows, :] = (exp_terms / total).astype(jnp.bfloat16)
        own_weight = (own_exp / total).astype(jnp.bfloat16).astype(jnp.float32)
        own_scr[part_rows, :] = own_weight * nv_ref[r : r + 1, :].astype(jnp.float32)
    own_scr[...] = jnp.dot(w_scr[...], v_ref[...], preferred_element_type=jnp.float32) + own_scr[...]
    for r in range(requests):
        for h in range(per_req):
            out_ref[r : r + 1, h * HD : (h + 1) * HD] = own_scr[r * per_req + h : r * per_req + h + 1, :]


def attend_pool(queries, new_key, new_value, key_pool, value_pool, lengths, page_table):
    row_count = queries.shape[0]
    pool_pages, page_rows, kv_width = key_pool.shape
    groups = kv_width // HD
    per_group = queries.shape[1] // kv_width
    pages_max = page_table.shape[1]
    pool_len = pool_pages * page_rows

    slot_start = lax.broadcasted_iota(jnp.int32, (row_count, pages_max), 1) * page_rows
    slot_live = slot_start < lengths[:, None]
    match = (page_table[:, :, None] == lax.broadcasted_iota(jnp.int32, (1, 1, pool_pages), 2)) & slot_live[
        :, :, None
    ]
    owned = jnp.any(match, axis=1)
    base = jnp.sum(jnp.where(match, slot_start[:, :, None], 0), axis=1)
    position = base[:, :, None] + lax.broadcasted_iota(jnp.int32, (1, 1, page_rows), 2)
    live_mask = (owned[:, :, None] & (position < lengths[:, None, None])).reshape(row_count, pool_len)

    key_rows = key_pool.reshape(pool_len, kv_width)
    value_rows = value_pool.reshape(pool_len, kv_width)
    n_rows = row_count * per_group
    group_cols = pl.BlockSpec((row_count, per_group * HD), lambda g: (0, g))
    lane_slice = pl.BlockSpec((pool_len, HD), lambda g: (0, g))
    new_slice = pl.BlockSpec((row_count, HD), lambda g: (0, g))
    summed = pl.pallas_call(
        softmax_kernel,
        grid=(groups,),
        out_shape=jax.ShapeDtypeStruct((row_count, groups * per_group * HD), jnp.float32),
        in_specs=[
            group_cols,
            lane_slice,
            lane_slice,
            pl.BlockSpec((row_count, pool_len), lambda g: (0, 0)),
            new_slice,
            new_slice,
        ],
        out_specs=group_cols,
        scratch_shapes=[
            pltpu.VMEM((n_rows, HD), queries.dtype),
            pltpu.VMEM((n_rows, pool_len), jnp.bfloat16),
            pltpu.VMEM((n_rows, HD), jnp.float32),
        ],
        interpret=INTERPRET,
    )(queries, key_rows, value_rows, live_mask.astype(jnp.int32), new_key, new_value)
    return summed.astype(jnp.bfloat16)


def gather_rows(block, n_req):
    copies = jnp.broadcast_to(block[None], (n_req,) + block.shape)
    gathered = lax.all_to_all(copies, "req", 0, 0, tiled=True)
    return gathered.reshape(n_req * block.shape[0], *block.shape[1:])


def body(
    queries,
    new_key,
    new_value,
    key_cache,
    value_cache,
    lengths,
    page_table,
    residual,
    out_weight,
    gate_weight,
    up_weight,
    down_weight,
):
    n_req = lax.axis_size("req")
    head = lax.axis_index("head")
    swap = [(0, 1), (1, 0)]
    half = out_weight.shape[0] // 2
    cols = out_weight.shape[1]

    partner_rows = lax.dynamic_slice_in_dim(out_weight, (1 - head) * half, half, axis=0)
    lent_rows = lax.ppermute(partner_rows, "head", swap)
    own_rows = lax.dynamic_slice_in_dim(out_weight, head * half, half, axis=0)

    attention = attend_pool(
        queries, new_key, new_value, key_cache, value_cache, lengths, page_table
    )
    features = gather_rows(attention, n_req)
    both = jnp.dot(
        features,
        jnp.concatenate([own_rows, lent_rows], axis=1),
        preferred_element_type=jnp.float32,
    )
    attn_update = both[:, :cols] + lax.ppermute(both[:, cols:], "head", swap)
    mixed_rows = (residual.astype(jnp.float32) + attn_update).astype(jnp.bfloat16)
    shard_piece = gather_rows(mixed_rows.T, n_req).reshape(n_req, *mixed_rows.T.shape)
    shard_piece = shard_piece.transpose(2, 0, 1).reshape(mixed_rows.shape[0], -1)
    gate_acts = jnp.dot(shard_piece, gate_weight, preferred_element_type=jnp.float32)
    up_acts = jnp.dot(shard_piece, up_weight, preferred_element_type=jnp.float32)
    acts = jnp.concatenate([gate_acts, up_acts], axis=1)
    acts = acts + lax.ppermute(acts, "head", swap)
    gate_full, up_full = jnp.split(acts, 2, axis=1)
    hidden = (jax.nn.silu(gate_full) * up_full).astype(jnp.bfloat16)
    pieces = jnp.einsum(
        "tf,fnc->ntc",
        hidden,
        down_weight.reshape(down_weight.shape[0], n_req, down_weight.shape[1] // n_req),
        preferred_element_type=jnp.float32,
    ).astype(jnp.bfloat16)
    gathered = lax.all_to_all(pieces, "req", 0, 0, tiled=True)
    down_part = jnp.sum(gathered.astype(jnp.float32), axis=0)
    return (mixed_rows.astype(jnp.float32) + down_part).astype(jnp.bfloat16)


def solution(mesh):
    return jax.shard_map(
        body,
        mesh=mesh,
        in_specs=(
            P("req", "head"),
            P("req", "head"),
            P("req", "head"),
            P("req", None, "head"),
            P("req", None, "head"),
            P("req"),
            P("req", None),
            P(None, ("head", "req")),
            P(None, ("head", "req")),
            P("head", "req"),
            P("head", "req"),
            P("req", "head"),
        ),
        out_specs=P(None, ("head", "req")),
        check_vma=False,
    )
```

```python
import jax
import jax.numpy as jnp
from jax import lax
from jax.experimental import pallas as pl
from jax.experimental.pallas import tpu as pltpu
from jax.sharding import PartitionSpec as P

HD = 128
INTERPRET = False


def softmax_kernel(q_ref, k_ref, v_ref, live_ref, nk_ref, nv_ref, out_ref, q_scr, w_scr, own_scr, att_scr):
    rows = q_scr.shape[0]
    requests = live_ref.shape[0]
    per_req = rows // requests
    for r in range(requests):
        for h in range(per_req):
            q_scr[r * per_req + h : r * per_req + h + 1, :] = q_ref[r : r + 1, h * HD : (h + 1) * HD]
    q = q_scr[...]
    scores = lax.dot_general(
        q, k_ref[...], (((1,), (1,)), ((), ())), preferred_element_type=jnp.float32
    ) * HD ** (-0.5)
    own_all = lax.dot_general(
        q, nk_ref[...], (((1,), (1,)), ((), ())), preferred_element_type=jnp.float32
    ) * HD ** (-0.5)
    for r in range(requests):
        part_rows = slice(r * per_req, (r + 1) * per_req)
        part = scores[part_rows, :]
        live = live_ref[r : r + 1, :] != 0
        own = own_all[part_rows, r : r + 1]
        top = jnp.maximum(jnp.max(jnp.where(live, part, -1e30), axis=1, keepdims=True), own)
        exp_terms = jnp.where(live, jnp.exp(part - top), 0.0)
        own_exp = jnp.exp(own - top)
        total = jnp.sum(exp_terms, axis=1, keepdims=True) + own_exp
        w_scr[part_rows, :] = (exp_terms / total).astype(jnp.bfloat16)
        own_weight = (own_exp / total).astype(jnp.bfloat16).astype(jnp.float32)
        own_scr[part_rows, :] = own_weight * nv_ref[r : r + 1, :].astype(jnp.float32)
    own_scr[...] = jnp.dot(w_scr[...], v_ref[...], preferred_element_type=jnp.float32) + own_scr[...]
    for r in range(requests):
        for h in range(per_req):
            att_scr[r : r + 1, h * HD : (h + 1) * HD] = own_scr[r * per_req + h : r * per_req + h + 1, :]
    out_ref[...] = jnp.broadcast_to(att_scr[...].astype(out_ref.dtype)[None], out_ref.shape)


def attend_pool(queries, new_key, new_value, key_pool, value_pool, lengths, page_table, copies):
    row_count = queries.shape[0]
    pool_pages, page_rows, kv_width = key_pool.shape
    groups = kv_width // HD
    per_group = queries.shape[1] // kv_width
    pages_max = page_table.shape[1]
    pool_len = pool_pages * page_rows

    slot_start = lax.broadcasted_iota(jnp.int32, (row_count, pages_max), 1) * page_rows
    slot_live = slot_start < lengths[:, None]
    match = (page_table[:, :, None] == lax.broadcasted_iota(jnp.int32, (1, 1, pool_pages), 2)) & slot_live[
        :, :, None
    ]
    owned = jnp.any(match, axis=1)
    base = jnp.sum(jnp.where(match, slot_start[:, :, None], 0), axis=1)
    position = base[:, :, None] + lax.broadcasted_iota(jnp.int32, (1, 1, page_rows), 2)
    live_mask = (owned[:, :, None] & (position < lengths[:, None, None])).reshape(row_count, pool_len)

    key_rows = key_pool.reshape(pool_len, kv_width)
    value_rows = value_pool.reshape(pool_len, kv_width)
    n_rows = row_count * per_group
    group_cols = pl.BlockSpec((row_count, per_group * HD), lambda g: (0, g))
    lane_slice = pl.BlockSpec((pool_len, HD), lambda g: (0, g))
    new_slice = pl.BlockSpec((row_count, HD), lambda g: (0, g))
    summed = pl.pallas_call(
        softmax_kernel,
        grid=(groups,),
        out_shape=jax.ShapeDtypeStruct((copies, row_count, groups * per_group * HD), jnp.bfloat16),
        in_specs=[
            group_cols,
            lane_slice,
            lane_slice,
            pl.BlockSpec((row_count, pool_len), lambda g: (0, 0)),
            new_slice,
            new_slice,
        ],
        out_specs=pl.BlockSpec((copies, row_count, per_group * HD), lambda g: (0, 0, g)),
        scratch_shapes=[
            pltpu.VMEM((n_rows, HD), queries.dtype),
            pltpu.VMEM((n_rows, pool_len), jnp.bfloat16),
            pltpu.VMEM((n_rows, HD), jnp.float32),
            pltpu.VMEM((row_count, per_group * HD), jnp.float32),
        ],
        interpret=INTERPRET,
    )(queries, key_rows, value_rows, live_mask.astype(jnp.int32), new_key, new_value)
    return summed


def gather_rows(block, n_req):
    copies = jnp.broadcast_to(block[None], (n_req,) + block.shape)
    gathered = lax.all_to_all(copies, "req", 0, 0, tiled=True)
    return gathered.reshape(n_req * block.shape[0], *block.shape[1:])


def body(
    queries,
    new_key,
    new_value,
    key_cache,
    value_cache,
    lengths,
    page_table,
    residual,
    out_weight,
    gate_weight,
    up_weight,
    down_weight,
):
    n_req = lax.axis_size("req")
    head = lax.axis_index("head")
    swap = [(0, 1), (1, 0)]
    half = out_weight.shape[0] // 2
    cols = out_weight.shape[1]

    partner_rows = lax.dynamic_slice_in_dim(out_weight, (1 - head) * half, half, axis=0)
    lent_rows = lax.ppermute(partner_rows, "head", swap)
    own_rows = lax.dynamic_slice_in_dim(out_weight, head * half, half, axis=0)

    attention_copies = attend_pool(
        queries, new_key, new_value, key_cache, value_cache, lengths, page_table, n_req
    )
    features = lax.all_to_all(attention_copies, "req", 0, 0, tiled=True).reshape(
        -1, attention_copies.shape[2]
    )
    both = jnp.dot(
        features,
        jnp.concatenate([own_rows, lent_rows], axis=1),
        preferred_element_type=jnp.float32,
    )
    attn_update = both[:, :cols] + lax.ppermute(both[:, cols:], "head", swap)
    mixed_rows = (residual.astype(jnp.float32) + attn_update).astype(jnp.bfloat16)
    shard_piece = gather_rows(mixed_rows.T, n_req).reshape(n_req, *mixed_rows.T.shape)
    shard_piece = shard_piece.transpose(2, 0, 1).reshape(mixed_rows.shape[0], -1)
    gate_acts = jnp.dot(shard_piece, gate_weight, preferred_element_type=jnp.float32)
    up_acts = jnp.dot(shard_piece, up_weight, preferred_element_type=jnp.float32)
    acts = jnp.concatenate([gate_acts, up_acts], axis=1)
    acts = acts + lax.ppermute(acts, "head", swap)
    gate_full, up_full = jnp.split(acts, 2, axis=1)
    hidden = (jax.nn.silu(gate_full) * up_full).astype(jnp.bfloat16)
    pieces = jnp.einsum(
        "tf,fnc->ntc",
        hidden,
        down_weight.reshape(down_weight.shape[0], n_req, down_weight.shape[1] // n_req),
        preferred_element_type=jnp.float32,
    ).astype(jnp.bfloat16)
    gathered = lax.all_to_all(pieces, "req", 0, 0, tiled=True)
    down_part = jnp.sum(gathered.astype(jnp.float32), axis=0)
    return (mixed_rows.astype(jnp.float32) + down_part).astype(jnp.bfloat16)


def solution(mesh):
    return jax.shard_map(
        body,
        mesh=mesh,
        in_specs=(
            P("req", "head"),
            P("req", "head"),
            P("req", "head"),
            P("req", None, "head"),
            P("req", None, "head"),
            P("req"),
            P("req", None),
            P(None, ("head", "req")),
            P(None, ("head", "req")),
            P("head", "req"),
            P("head", "req"),
            P("req", "head"),
        ),
        out_specs=P(None, ("head", "req")),
        check_vma=False,
    )
```

```python
import jax
import jax.numpy as jnp
from jax import lax
from jax.experimental import pallas as pl
from jax.experimental.pallas import tpu as pltpu
from jax.sharding import PartitionSpec as P

HD = 128
INTERPRET = False


def softmax_kernel(q_ref, k_ref, v_ref, live_ref, nk_ref, nv_ref, out_ref, q_scr, w_scr, own_scr, att_scr):
    rows = q_scr.shape[0]
    requests = live_ref.shape[0]
    per_req = rows // requests
    for r in range(requests):
        for h in range(per_req):
            q_scr[r * per_req + h : r * per_req + h + 1, :] = q_ref[r : r + 1, h * HD : (h + 1) * HD]
    q = q_scr[...]
    scores = lax.dot_general(
        q, k_ref[...], (((1,), (1,)), ((), ())), preferred_element_type=jnp.float32
    ) * HD ** (-0.5)
    own_all = lax.dot_general(
        q, nk_ref[...], (((1,), (1,)), ((), ())), preferred_element_type=jnp.float32
    ) * HD ** (-0.5)
    for r in range(requests):
        part_rows = slice(r * per_req, (r + 1) * per_req)
        part = scores[part_rows, :]
        live = live_ref[r : r + 1, :] != 0
        own = own_all[part_rows, r : r + 1]
        top = jnp.maximum(jnp.max(jnp.where(live, part, -1e30), axis=1, keepdims=True), own)
        exp_terms = jnp.where(live, jnp.exp(part - top), 0.0)
        own_exp = jnp.exp(own - top)
        total = jnp.sum(exp_terms, axis=1, keepdims=True) + own_exp
        w_scr[part_rows, :] = (exp_terms / total).astype(jnp.bfloat16)
        own_weight = (own_exp / total).astype(jnp.bfloat16).astype(jnp.float32)
        own_scr[part_rows, :] = own_weight * nv_ref[r : r + 1, :].astype(jnp.float32)
    own_scr[...] = jnp.dot(w_scr[...], v_ref[...], preferred_element_type=jnp.float32) + own_scr[...]
    for r in range(requests):
        for h in range(per_req):
            att_scr[r : r + 1, h * HD : (h + 1) * HD] = own_scr[r * per_req + h : r * per_req + h + 1, :]
    out_ref[...] = jnp.broadcast_to(att_scr[...].astype(out_ref.dtype)[None], out_ref.shape)


def attend_pool(queries, new_key, new_value, key_pool, value_pool, lengths, page_table, copies):
    row_count = queries.shape[0]
    pool_pages, page_rows, kv_width = key_pool.shape
    groups = kv_width // HD
    per_group = queries.shape[1] // kv_width
    pages_max = page_table.shape[1]
    pool_len = pool_pages * page_rows

    slot_ids = lax.broadcasted_iota(jnp.int32, (row_count, pages_max, pool_pages), 1)
    named = page_table[:, :, None] == lax.broadcasted_iota(jnp.int32, (1, 1, pool_pages), 2)
    slot_of = jnp.min(jnp.where(named, slot_ids, pages_max), axis=1)
    position = slot_of[:, :, None] * page_rows + lax.broadcasted_iota(jnp.int32, (1, 1, page_rows), 2)
    live_mask = (position < lengths[:, None, None]).reshape(row_count, pool_len)

    key_rows = key_pool.reshape(pool_len, kv_width)
    value_rows = value_pool.reshape(pool_len, kv_width)
    n_rows = row_count * per_group
    group_cols = pl.BlockSpec((row_count, per_group * HD), lambda g: (0, g))
    lane_slice = pl.BlockSpec((pool_len, HD), lambda g: (0, g))
    new_slice = pl.BlockSpec((row_count, HD), lambda g: (0, g))
    summed = pl.pallas_call(
        softmax_kernel,
        grid=(groups,),
        out_shape=jax.ShapeDtypeStruct((copies, row_count, groups * per_group * HD), jnp.bfloat16),
        in_specs=[
            group_cols,
            lane_slice,
            lane_slice,
            pl.BlockSpec((row_count, pool_len), lambda g: (0, 0)),
            new_slice,
            new_slice,
        ],
        out_specs=pl.BlockSpec((copies, row_count, per_group * HD), lambda g: (0, 0, g)),
        scratch_shapes=[
            pltpu.VMEM((n_rows, HD), queries.dtype),
            pltpu.VMEM((n_rows, pool_len), jnp.bfloat16),
            pltpu.VMEM((n_rows, HD), jnp.float32),
            pltpu.VMEM((row_count, per_group * HD), jnp.float32),
        ],
        interpret=INTERPRET,
    )(queries, key_rows, value_rows, live_mask.astype(jnp.int32), new_key, new_value)
    return summed


def gather_rows(block, n_req):
    copies = jnp.broadcast_to(block[None], (n_req,) + block.shape)
    gathered = lax.all_to_all(copies, "req", 0, 0, tiled=True)
    return gathered.reshape(n_req * block.shape[0], *block.shape[1:])


def body(
    queries,
    new_key,
    new_value,
    key_cache,
    value_cache,
    lengths,
    page_table,
    residual,
    out_weight,
    gate_weight,
    up_weight,
    down_weight,
):
    n_req = lax.axis_size("req")
    head = lax.axis_index("head")
    swap = [(0, 1), (1, 0)]
    half = out_weight.shape[0] // 2
    cols = out_weight.shape[1]

    partner_rows = lax.dynamic_slice_in_dim(out_weight, (1 - head) * half, half, axis=0)
    lent_rows = lax.ppermute(partner_rows, "head", swap)
    own_rows = lax.dynamic_slice_in_dim(out_weight, head * half, half, axis=0)

    attention_copies = attend_pool(
        queries, new_key, new_value, key_cache, value_cache, lengths, page_table, n_req
    )
    features = lax.all_to_all(attention_copies, "req", 0, 0, tiled=True).reshape(
        -1, attention_copies.shape[2]
    )
    both = jnp.dot(
        features,
        jnp.concatenate([own_rows, lent_rows], axis=1),
        preferred_element_type=jnp.float32,
    )
    attn_update = both[:, :cols] + lax.ppermute(both[:, cols:], "head", swap)
    mixed_rows = (residual.astype(jnp.float32) + attn_update).astype(jnp.bfloat16)
    shard_piece = gather_rows(mixed_rows.T, n_req).reshape(n_req, *mixed_rows.T.shape)
    shard_piece = shard_piece.transpose(2, 0, 1).reshape(mixed_rows.shape[0], -1)
    gate_acts = jnp.dot(shard_piece, gate_weight, preferred_element_type=jnp.float32)
    up_acts = jnp.dot(shard_piece, up_weight, preferred_element_type=jnp.float32)
    acts = jnp.concatenate([gate_acts, up_acts], axis=1)
    acts = acts + lax.ppermute(acts, "head", swap)
    gate_full, up_full = jnp.split(acts, 2, axis=1)
    hidden = (jax.nn.silu(gate_full) * up_full).astype(jnp.bfloat16)
    pieces = jnp.einsum(
        "tf,fnc->ntc",
        hidden,
        down_weight.reshape(down_weight.shape[0], n_req, down_weight.shape[1] // n_req),
        preferred_element_type=jnp.float32,
    ).astype(jnp.bfloat16)
    gathered = lax.all_to_all(pieces, "req", 0, 0, tiled=True)
    down_part = jnp.sum(gathered.astype(jnp.float32), axis=0)
    return (mixed_rows.astype(jnp.float32) + down_part).astype(jnp.bfloat16)


def solution(mesh):
    return jax.shard_map(
        body,
        mesh=mesh,
        in_specs=(
            P("req", "head"),
            P("req", "head"),
            P("req", "head"),
            P("req", None, "head"),
            P("req", None, "head"),
            P("req"),
            P("req", None),
            P(None, ("head", "req")),
            P(None, ("head", "req")),
            P("head", "req"),
            P("head", "req"),
            P("req", "head"),
        ),
        out_specs=P(None, ("head", "req")),
        check_vma=False,
    )
```

```python
import jax
import jax.numpy as jnp
from jax import lax
from jax.experimental import pallas as pl
from jax.experimental.pallas import tpu as pltpu
from jax.sharding import PartitionSpec as P

HD = 128
INTERPRET = False


def softmax_kernel(q_ref, k_ref, v_ref, live_ref, nk_ref, nv_ref, out_ref, q_scr, w_scr, own_scr, att_scr):
    rows = q_scr.shape[0]
    requests = live_ref.shape[0]
    per_req = rows // requests
    for r in range(requests):
        for h in range(per_req):
            q_scr[r * per_req + h : r * per_req + h + 1, :] = q_ref[r : r + 1, h * HD : (h + 1) * HD]
    q = q_scr[...]
    scores = lax.dot_general(
        q, k_ref[...], (((1,), (1,)), ((), ())), preferred_element_type=jnp.float32
    ) * HD ** (-0.5)
    own_all = lax.dot_general(
        q, nk_ref[...], (((1,), (1,)), ((), ())), preferred_element_type=jnp.float32
    ) * HD ** (-0.5)
    for r in range(requests):
        part_rows = slice(r * per_req, (r + 1) * per_req)
        part = scores[part_rows, :]
        live = live_ref[r : r + 1, :] != 0
        own = own_all[part_rows, r : r + 1]
        top = jnp.maximum(jnp.max(jnp.where(live, part, -1e30), axis=1, keepdims=True), own)
        exp_terms = jnp.where(live, jnp.exp(part - top), 0.0)
        own_exp = jnp.exp(own - top)
        total = jnp.sum(exp_terms, axis=1, keepdims=True) + own_exp
        w_scr[part_rows, :] = (exp_terms / total).astype(jnp.bfloat16)
        own_weight = (own_exp / total).astype(jnp.bfloat16).astype(jnp.float32)
        own_scr[part_rows, :] = own_weight * nv_ref[r : r + 1, :].astype(jnp.float32)
    own_scr[...] = jnp.dot(w_scr[...], v_ref[...], preferred_element_type=jnp.float32) + own_scr[...]
    for r in range(requests):
        for h in range(per_req):
            att_scr[r : r + 1, h * HD : (h + 1) * HD] = own_scr[r * per_req + h : r * per_req + h + 1, :]
    out_ref[...] = jnp.broadcast_to(att_scr[...].astype(out_ref.dtype)[None], out_ref.shape)


def attend_pool(queries, new_key, new_value, key_pool, value_pool, lengths, page_table, copies):
    row_count = queries.shape[0]
    pool_pages, page_rows, kv_width = key_pool.shape
    groups = kv_width // HD
    per_group = queries.shape[1] // kv_width
    pages_max = page_table.shape[1]
    pool_len = pool_pages * page_rows

    slot_ids = lax.broadcasted_iota(jnp.int32, (row_count, pages_max, pool_pages), 1)
    named = page_table[:, :, None] == lax.broadcasted_iota(jnp.int32, (1, 1, pool_pages), 2)
    slot_of = jnp.min(jnp.where(named, slot_ids, pages_max), axis=1)
    position = slot_of[:, :, None] * page_rows + lax.broadcasted_iota(jnp.int32, (1, 1, page_rows), 2)
    live_mask = (position < lengths[:, None, None]).reshape(row_count, pool_len)

    key_rows = key_pool.reshape(pool_len, kv_width)
    value_rows = value_pool.reshape(pool_len, kv_width)
    n_rows = row_count * per_group
    group_cols = pl.BlockSpec((row_count, per_group * HD), lambda g: (0, g))
    lane_slice = pl.BlockSpec((pool_len, HD), lambda g: (0, g))
    new_slice = pl.BlockSpec((row_count, HD), lambda g: (0, g))
    summed = pl.pallas_call(
        softmax_kernel,
        grid=(groups,),
        out_shape=jax.ShapeDtypeStruct((copies, row_count, groups * per_group * HD), jnp.bfloat16),
        in_specs=[
            group_cols,
            lane_slice,
            lane_slice,
            pl.BlockSpec((row_count, pool_len), lambda g: (0, 0)),
            new_slice,
            new_slice,
        ],
        out_specs=pl.BlockSpec((copies, row_count, per_group * HD), lambda g: (0, 0, g)),
        scratch_shapes=[
            pltpu.VMEM((n_rows, HD), queries.dtype),
            pltpu.VMEM((n_rows, pool_len), jnp.bfloat16),
            pltpu.VMEM((n_rows, HD), jnp.float32),
            pltpu.VMEM((row_count, per_group * HD), jnp.float32),
        ],
        interpret=INTERPRET,
    )(queries, key_rows, value_rows, live_mask.astype(jnp.int32), new_key, new_value)
    return summed


def gather_rows(block, n_req):
    copies = jnp.broadcast_to(block[None], (n_req,) + block.shape)
    gathered = lax.all_to_all(copies, "req", 0, 0, tiled=True)
    return gathered.reshape(n_req * block.shape[0], *block.shape[1:])


def body(
    queries,
    new_key,
    new_value,
    key_cache,
    value_cache,
    lengths,
    page_table,
    residual,
    out_weight,
    gate_weight,
    up_weight,
    down_weight,
):
    n_req = lax.axis_size("req")
    head = lax.axis_index("head")
    swap = [(0, 1), (1, 0)]
    half = out_weight.shape[0] // 2
    cols = out_weight.shape[1]

    partner_rows = lax.dynamic_slice_in_dim(out_weight, (1 - head) * half, half, axis=0)
    lent_rows = lax.ppermute(partner_rows, "head", swap)
    own_rows = lax.dynamic_slice_in_dim(out_weight, head * half, half, axis=0)

    attention_copies = attend_pool(
        queries, new_key, new_value, key_cache, value_cache, lengths, page_table, n_req
    )
    features = lax.all_to_all(attention_copies, "req", 0, 0, tiled=True).reshape(
        -1, attention_copies.shape[2]
    )
    both_rows = lax.optimization_barrier(jnp.concatenate([own_rows, lent_rows], axis=1))
    both = jnp.dot(features, both_rows, preferred_element_type=jnp.float32)
    attn_update = both[:, :cols] + lax.ppermute(both[:, cols:], "head", swap)
    mixed_rows = (residual.astype(jnp.float32) + attn_update).astype(jnp.bfloat16)
    shard_piece = gather_rows(mixed_rows.T, n_req).reshape(n_req, *mixed_rows.T.shape)
    shard_piece = shard_piece.transpose(2, 0, 1).reshape(mixed_rows.shape[0], -1)
    gate_acts = jnp.dot(shard_piece, gate_weight, preferred_element_type=jnp.float32)
    up_acts = jnp.dot(shard_piece, up_weight, preferred_element_type=jnp.float32)
    acts = jnp.concatenate([gate_acts, up_acts], axis=1)
    acts = acts + lax.ppermute(acts, "head", swap)
    gate_full, up_full = jnp.split(acts, 2, axis=1)
    hidden = (jax.nn.silu(gate_full) * up_full).astype(jnp.bfloat16)
    pieces = jnp.einsum(
        "tf,fnc->ntc",
        hidden,
        down_weight.reshape(down_weight.shape[0], n_req, down_weight.shape[1] // n_req),
        preferred_element_type=jnp.float32,
    ).astype(jnp.bfloat16)
    gathered = lax.all_to_all(pieces, "req", 0, 0, tiled=True)
    down_part = jnp.sum(gathered.astype(jnp.float32), axis=0)
    return (mixed_rows.astype(jnp.float32) + down_part).astype(jnp.bfloat16)


def solution(mesh):
    return jax.shard_map(
        body,
        mesh=mesh,
        in_specs=(
            P("req", "head"),
            P("req", "head"),
            P("req", "head"),
            P("req", None, "head"),
            P("req", None, "head"),
            P("req"),
            P("req", None),
            P(None, ("head", "req")),
            P(None, ("head", "req")),
            P("head", "req"),
            P("head", "req"),
            P("req", "head"),
        ),
        out_specs=P(None, ("head", "req")),
        check_vma=False,
    )
```

```python
import jax
import jax.numpy as jnp
from jax import lax
from jax.experimental import pallas as pl
from jax.experimental.pallas import tpu as pltpu
from jax.sharding import PartitionSpec as P

HD = 128
INTERPRET = False


def softmax_kernel(q_ref, k_ref, v_ref, live_ref, nk_ref, nv_ref, out_ref, q_scr, w_scr, own_scr, att_scr):
    rows = q_scr.shape[0]
    requests = live_ref.shape[0]
    per_req = rows // requests
    for r in range(requests):
        for h in range(per_req):
            q_scr[r * per_req + h : r * per_req + h + 1, :] = q_ref[r : r + 1, h * HD : (h + 1) * HD]
    q = q_scr[...]
    scores = lax.dot_general(
        q, k_ref[...], (((1,), (1,)), ((), ())), preferred_element_type=jnp.float32
    ) * HD ** (-0.5)
    own_all = lax.dot_general(
        q, nk_ref[...], (((1,), (1,)), ((), ())), preferred_element_type=jnp.float32
    ) * HD ** (-0.5)
    for r in range(requests):
        part_rows = slice(r * per_req, (r + 1) * per_req)
        part = scores[part_rows, :]
        live = live_ref[r : r + 1, :] != 0
        own = own_all[part_rows, r : r + 1]
        top = jnp.maximum(jnp.max(jnp.where(live, part, -1e30), axis=1, keepdims=True), own)
        exp_terms = jnp.where(live, jnp.exp(part - top), 0.0)
        own_exp = jnp.exp(own - top)
        total = jnp.sum(exp_terms, axis=1, keepdims=True) + own_exp
        w_scr[part_rows, :] = (exp_terms / total).astype(jnp.bfloat16)
        own_weight = (own_exp / total).astype(jnp.bfloat16).astype(jnp.float32)
        own_scr[part_rows, :] = own_weight * nv_ref[r : r + 1, :].astype(jnp.float32)
    own_scr[...] = jnp.dot(w_scr[...], v_ref[...], preferred_element_type=jnp.float32) + own_scr[...]
    for r in range(requests):
        for h in range(per_req):
            att_scr[r : r + 1, h * HD : (h + 1) * HD] = own_scr[r * per_req + h : r * per_req + h + 1, :]
    out_ref[...] = jnp.broadcast_to(att_scr[...].astype(out_ref.dtype)[None], out_ref.shape)


def attend_pool(queries, new_key, new_value, key_pool, value_pool, lengths, page_table, copies):
    row_count = queries.shape[0]
    pool_pages, page_rows, kv_width = key_pool.shape
    groups = kv_width // HD
    per_group = queries.shape[1] // kv_width
    pages_max = page_table.shape[1]
    pool_len = pool_pages * page_rows

    slot_ids = lax.broadcasted_iota(jnp.int32, (row_count, pages_max, pool_pages), 1)
    named = page_table[:, :, None] == lax.broadcasted_iota(jnp.int32, (1, 1, pool_pages), 2)
    slot_of = jnp.min(jnp.where(named, slot_ids, pages_max), axis=1)
    position = slot_of[:, :, None] * page_rows + lax.broadcasted_iota(jnp.int32, (1, 1, page_rows), 2)
    live_mask = (position < lengths[:, None, None]).reshape(row_count, pool_len)

    key_rows = key_pool.reshape(pool_len, kv_width)
    value_rows = value_pool.reshape(pool_len, kv_width)
    n_rows = row_count * per_group
    group_cols = pl.BlockSpec((row_count, per_group * HD), lambda g: (0, g))
    lane_slice = pl.BlockSpec((pool_len, HD), lambda g: (0, g))
    new_slice = pl.BlockSpec((row_count, HD), lambda g: (0, g))
    summed = pl.pallas_call(
        softmax_kernel,
        grid=(groups,),
        out_shape=jax.ShapeDtypeStruct((copies, row_count, groups * per_group * HD), jnp.bfloat16),
        in_specs=[
            group_cols,
            lane_slice,
            lane_slice,
            pl.BlockSpec((row_count, pool_len), lambda g: (0, 0)),
            new_slice,
            new_slice,
        ],
        out_specs=pl.BlockSpec((copies, row_count, per_group * HD), lambda g: (0, 0, g)),
        scratch_shapes=[
            pltpu.VMEM((n_rows, HD), queries.dtype),
            pltpu.VMEM((n_rows, pool_len), jnp.bfloat16),
            pltpu.VMEM((n_rows, HD), jnp.float32),
            pltpu.VMEM((row_count, per_group * HD), jnp.float32),
        ],
        interpret=INTERPRET,
    )(queries, key_rows, value_rows, live_mask.astype(jnp.int32), new_key, new_value)
    return summed


def gather_rows(block, n_req):
    copies = jnp.broadcast_to(block[None], (n_req,) + block.shape)
    gathered = lax.all_to_all(copies, "req", 0, 0, tiled=True)
    return gathered.reshape(n_req * block.shape[0], *block.shape[1:])


def body(
    queries,
    new_key,
    new_value,
    key_cache,
    value_cache,
    lengths,
    page_table,
    residual,
    out_weight,
    gate_weight,
    up_weight,
    down_weight,
):
    n_req = lax.axis_size("req")
    head = lax.axis_index("head")
    swap = [(0, 1), (1, 0)]
    half = out_weight.shape[0] // 2
    cols = out_weight.shape[1]

    partner_rows = lax.dynamic_slice_in_dim(out_weight, (1 - head) * half, half, axis=0)
    lent_rows = lax.ppermute(partner_rows, "head", swap)
    own_rows = lax.dynamic_slice_in_dim(out_weight, head * half, half, axis=0)

    attention_copies = attend_pool(
        queries, new_key, new_value, key_cache, value_cache, lengths, page_table, n_req
    )
    features = lax.all_to_all(attention_copies, "req", 0, 0, tiled=True).reshape(
        -1, attention_copies.shape[2]
    )
    for_partner = jnp.dot(features, lent_rows, preferred_element_type=jnp.float32)
    from_partner = lax.ppermute(for_partner, "head", swap)
    attn_update = jnp.dot(features, own_rows, preferred_element_type=jnp.float32) + from_partner
    mixed_rows = (residual.astype(jnp.float32) + attn_update).astype(jnp.bfloat16)
    shard_piece = gather_rows(mixed_rows.T, n_req).reshape(n_req, *mixed_rows.T.shape)
    shard_piece = shard_piece.transpose(2, 0, 1).reshape(mixed_rows.shape[0], -1)
    gate_acts = jnp.dot(shard_piece, gate_weight, preferred_element_type=jnp.float32)
    up_acts = jnp.dot(shard_piece, up_weight, preferred_element_type=jnp.float32)
    acts = jnp.concatenate([gate_acts, up_acts], axis=1)
    acts = acts + lax.ppermute(acts, "head", swap)
    gate_full, up_full = jnp.split(acts, 2, axis=1)
    hidden = (jax.nn.silu(gate_full) * up_full).astype(jnp.bfloat16)
    pieces = jnp.einsum(
        "tf,fnc->ntc",
        hidden,
        down_weight.reshape(down_weight.shape[0], n_req, down_weight.shape[1] // n_req),
        preferred_element_type=jnp.float32,
    ).astype(jnp.bfloat16)
    gathered = lax.all_to_all(pieces, "req", 0, 0, tiled=True)
    down_part = jnp.sum(gathered.astype(jnp.float32), axis=0)
    return (mixed_rows.astype(jnp.float32) + down_part).astype(jnp.bfloat16)


def solution(mesh):
    return jax.shard_map(
        body,
        mesh=mesh,
        in_specs=(
            P("req", "head"),
            P("req", "head"),
            P("req", "head"),
            P("req", None, "head"),
            P("req", None, "head"),
            P("req"),
            P("req", None),
            P(None, ("head", "req")),
            P(None, ("head", "req")),
            P("head", "req"),
            P("head", "req"),
            P("req", "head"),
        ),
        out_specs=P(None, ("head", "req")),
        check_vma=False,
    )
```

```python
import jax
import jax.numpy as jnp
from jax import lax
from jax.experimental import pallas as pl
from jax.experimental.pallas import tpu as pltpu
from jax.sharding import PartitionSpec as P

HD = 128
INTERPRET = False


def softmax_kernel(q_ref, k_ref, v_ref, live_ref, nk_ref, nv_ref, out_ref, q_scr, w_scr, own_scr, att_scr):
    rows = q_scr.shape[0]
    requests = live_ref.shape[0]
    per_req = rows // requests
    for r in range(requests):
        for h in range(per_req):
            q_scr[r * per_req + h : r * per_req + h + 1, :] = q_ref[r : r + 1, h * HD : (h + 1) * HD]
    q = q_scr[...]
    scores = lax.dot_general(
        q, k_ref[...], (((1,), (1,)), ((), ())), preferred_element_type=jnp.float32
    ) * HD ** (-0.5)
    own_all = lax.dot_general(
        q, nk_ref[...], (((1,), (1,)), ((), ())), preferred_element_type=jnp.float32
    ) * HD ** (-0.5)
    for r in range(requests):
        part_rows = slice(r * per_req, (r + 1) * per_req)
        part = scores[part_rows, :]
        live = live_ref[r : r + 1, :] != 0
        own = own_all[part_rows, r : r + 1]
        top = jnp.maximum(jnp.max(jnp.where(live, part, -1e30), axis=1, keepdims=True), own)
        exp_terms = jnp.where(live, jnp.exp(part - top), 0.0)
        own_exp = jnp.exp(own - top)
        total = jnp.sum(exp_terms, axis=1, keepdims=True) + own_exp
        w_scr[part_rows, :] = (exp_terms / total).astype(jnp.bfloat16)
        own_weight = (own_exp / total).astype(jnp.bfloat16).astype(jnp.float32)
        own_scr[part_rows, :] = own_weight * nv_ref[r : r + 1, :].astype(jnp.float32)
    own_scr[...] = jnp.dot(w_scr[...], v_ref[...], preferred_element_type=jnp.float32) + own_scr[...]
    for r in range(requests):
        for h in range(per_req):
            att_scr[r : r + 1, h * HD : (h + 1) * HD] = own_scr[r * per_req + h : r * per_req + h + 1, :]
    out_ref[...] = jnp.broadcast_to(att_scr[...].astype(out_ref.dtype)[None], out_ref.shape)


def attend_pool(queries, new_key, new_value, key_pool, value_pool, lengths, page_table, copies):
    row_count = queries.shape[0]
    pool_pages, page_rows, kv_width = key_pool.shape
    groups = kv_width // HD
    per_group = queries.shape[1] // kv_width
    pages_max = page_table.shape[1]
    pool_len = pool_pages * page_rows

    slot_ids = lax.broadcasted_iota(jnp.int32, (row_count, pages_max, pool_pages), 1)
    named = page_table[:, :, None] == lax.broadcasted_iota(jnp.int32, (1, 1, pool_pages), 2)
    slot_of = jnp.min(jnp.where(named, slot_ids, pages_max), axis=1)
    position = slot_of[:, :, None] * page_rows + lax.broadcasted_iota(jnp.int32, (1, 1, page_rows), 2)
    live_mask = (position < lengths[:, None, None]).reshape(row_count, pool_len)

    key_rows = key_pool.reshape(pool_len, kv_width)
    value_rows = value_pool.reshape(pool_len, kv_width)
    n_rows = row_count * per_group
    group_cols = pl.BlockSpec((row_count, per_group * HD), lambda g: (0, g))
    lane_slice = pl.BlockSpec((pool_len, HD), lambda g: (0, g))
    new_slice = pl.BlockSpec((row_count, HD), lambda g: (0, g))
    summed = pl.pallas_call(
        softmax_kernel,
        grid=(groups,),
        out_shape=jax.ShapeDtypeStruct((copies, row_count, groups * per_group * HD), jnp.bfloat16),
        in_specs=[
            group_cols,
            lane_slice,
            lane_slice,
            pl.BlockSpec((row_count, pool_len), lambda g: (0, 0)),
            new_slice,
            new_slice,
        ],
        out_specs=pl.BlockSpec((copies, row_count, per_group * HD), lambda g: (0, 0, g)),
        scratch_shapes=[
            pltpu.VMEM((n_rows, HD), queries.dtype),
            pltpu.VMEM((n_rows, pool_len), jnp.bfloat16),
            pltpu.VMEM((n_rows, HD), jnp.float32),
            pltpu.VMEM((row_count, per_group * HD), jnp.float32),
        ],
        interpret=INTERPRET,
    )(queries, key_rows, value_rows, live_mask.astype(jnp.int32), new_key, new_value)
    return summed


def gather_rows(block, n_req):
    copies = jnp.broadcast_to(block[None], (n_req,) + block.shape)
    gathered = lax.all_to_all(copies, "req", 0, 0, tiled=True)
    return gathered.reshape(n_req * block.shape[0], *block.shape[1:])


def body(
    queries,
    new_key,
    new_value,
    key_cache,
    value_cache,
    lengths,
    page_table,
    residual,
    out_weight,
    gate_weight,
    up_weight,
    down_weight,
):
    n_req = lax.axis_size("req")
    head = lax.axis_index("head")
    swap = [(0, 1), (1, 0)]
    half = out_weight.shape[0] // 2
    cols = out_weight.shape[1]

    partner_rows = lax.dynamic_slice_in_dim(out_weight, (1 - head) * half, half, axis=0)
    lent_rows = lax.ppermute(partner_rows, "head", swap)
    own_rows = lax.dynamic_slice_in_dim(out_weight, head * half, half, axis=0)

    attention_copies = attend_pool(
        queries, new_key, new_value, key_cache, value_cache, lengths, page_table, n_req
    )
    features = lax.all_to_all(attention_copies, "req", 0, 0, tiled=True).reshape(
        -1, attention_copies.shape[2]
    )
    both = jnp.dot(
        features,
        jnp.concatenate([own_rows, lent_rows], axis=1),
        preferred_element_type=jnp.float32,
    )
    attn_update = both[:, :cols] + lax.ppermute(both[:, cols:], "head", swap)
    mixed_rows = (residual.astype(jnp.float32) + attn_update).astype(jnp.bfloat16)
    shard_piece = gather_rows(mixed_rows, n_req).reshape(n_req, *mixed_rows.shape)
    shard_piece = shard_piece.transpose(1, 0, 2).reshape(mixed_rows.shape[0], -1)
    gate_acts = jnp.dot(shard_piece, gate_weight, preferred_element_type=jnp.float32)
    up_acts = jnp.dot(shard_piece, up_weight, preferred_element_type=jnp.float32)
    acts = jnp.concatenate([gate_acts, up_acts], axis=1)
    acts = acts + lax.ppermute(acts, "head", swap)
    gate_full, up_full = jnp.split(acts, 2, axis=1)
    hidden = (jax.nn.silu(gate_full) * up_full).astype(jnp.bfloat16)
    pieces = jnp.einsum(
        "tf,fnc->ntc",
        hidden,
        down_weight.reshape(down_weight.shape[0], n_req, down_weight.shape[1] // n_req),
        preferred_element_type=jnp.float32,
    ).astype(jnp.bfloat16)
    gathered = lax.all_to_all(pieces, "req", 0, 0, tiled=True)
    down_part = jnp.sum(gathered.astype(jnp.float32), axis=0)
    return (mixed_rows.astype(jnp.float32) + down_part).astype(jnp.bfloat16)


def solution(mesh):
    return jax.shard_map(
        body,
        mesh=mesh,
        in_specs=(
            P("req", "head"),
            P("req", "head"),
            P("req", "head"),
            P("req", None, "head"),
            P("req", None, "head"),
            P("req"),
            P("req", None),
            P(None, ("head", "req")),
            P(None, ("head", "req")),
            P("head", "req"),
            P("head", "req"),
            P("req", "head"),
        ),
        out_specs=P(None, ("head", "req")),
        check_vma=False,
    )
```
